512 devices in a mesh: freq: 8 (over x, core), geo: 64 (over z, y).
Axes of the slice: x: 4, y: 8, z: 8, core: 2. Of those that a mesh axis runs over, the one named last changes fastest.
Arguments:
- energy: float32 [256, 48, 36, 128], P('geo', 'freq'), may hold values from 0.1 to 1.5
- water_depth: float32 [256, 128], P('geo'), may hold values from 0.5 to 4
- wet_mask: int32 [256, 128], P('geo'), may hold values 0 or 1
- vegetation: int32 [256, 128], P('geo'), may hold values 0 or 1
- canopy: float32 [256, 128], P('geo'), may hold values from 0.004 to 0.04
- quad_offsets: int32 [4], replicated, may hold values from 1 to 3, as said below
- quad_weights: float32 [2], replicated, may hold values from 0.2 to 0.8
Outputs:
- energy_next: float32 [256, 48, 36, 128], P('geo', 'freq')
- orbital: float32 [256, 128], P('geo')
The draws below stay inside these ranges and needn't reach their ends.
Inputs may be any that keep to these rules, and one draw needn't show every extreme that they name: `quad_offsets`: offsets a and the two direction turns lie in 1 .. 3; the lower frequency offset b equals 3 in every draw.
All inputs are finite; a program needn't handle non-finite values. No bound on the sum of `wet_mask` or of `vegetation` on one device may be relied on, other than what follows from the above.
Results may differ from the reference program's by a relative error of at most 0.00002.
Values sent between devices are 32-bit elements; how exact they have to be, the bound alone decides.
No kernel may reach another device: no remote copies, remote signals or barrier semaphores. Data moves between devices by JAX's collectives and lax.ppermute only.
A program may use at most 64 MiB of HBM per device.

```python
import math
import jax
import jax.numpy as jnp
from jax import lax

FREQS = 48
DIRS = 36
FH = 4
SUBSTEPS = 8
CY = 4
NX = 128
NY = 256


def draw_quad_offsets(key, part):
    keys = jax.random.split(key, 2)
    up_bins = jax.random.randint(keys[0], (1,), 1, FH)
    down_bins = jnp.full((1,), FH - 1, jnp.int32)
    turns = jax.random.randint(keys[1], (2,), 1, FH)
    return jnp.concatenate([up_bins, down_bins, turns]).astype(jnp.int32)


def touch_ends(values, rng, low, high):
    dims = values.shape
    place = [jax.random.randint(jax.random.fold_in(rng, axis), (), 0, dims[axis]) for axis in range(len(dims))]
    values = values.at[tuple(place)].set(low)
    longest = dims.index(max(dims))
    place[longest] = (place[longest] + 1) % dims[longest]
    return values.at[tuple(place)].set(high)


def shard_levels(own_key, dims, shards, low, high):
    gain, own = 1.0, jax.random.fold_in(own_key, 6)
    for axis_at, shards_of in shards:
        steps = jnp.exp(jax.random.uniform(jax.random.fold_in(own, axis_at), (shards_of,), jnp.float32, low / len(shards), high / len(shards)))
        gain = gain * jnp.repeat(steps, dims[axis_at] // shards_of).reshape([-1 if axis == axis_at else 1 for axis in range(len(dims))])
    return gain


def setup_inputs(seed: int = 0) -> dict:
    arg_keys = jax.random.split(jax.random.key(seed), 8)
    return {
        "energy": jnp.clip(jnp.exp(math.log(1.5) - 2.7080502 * jax.random.uniform(arg_keys[0], (NY, FREQS, DIRS, NX), jnp.float32) ** shard_levels(arg_keys[0], (NY, FREQS, DIRS, NX), ((0, 64), (1, 8)), -0.2, 0.2)), 0.1, 1.5),
        "water_depth": jnp.clip(0.5 + 3.5 * jax.random.uniform(arg_keys[1], (NY, NX), jnp.float32) ** shard_levels(arg_keys[1], (NY, NX), ((0, 64),), -0.2, 0.2), 0.5, 4.0),
        "wet_mask": touch_ends((jax.random.randint(arg_keys[2], (NY, NX), 0, 5) < 4).astype(jnp.int32), jax.random.fold_in(arg_keys[2], 1), 0, 1),
        "vegetation": touch_ends((jax.random.randint(arg_keys[3], (NY, NX), 0, 2) < 1).astype(jnp.int32), jax.random.fold_in(arg_keys[3], 1), 0, 1),
        "canopy": jnp.clip(jnp.exp(math.log(0.04) - 2.30258502 * jax.random.uniform(arg_keys[4], (NY, NX), jnp.float32) ** shard_levels(arg_keys[4], (NY, NX), ((0, 64),), -0.2, 0.2)), 0.004, 0.04),
        "quad_offsets": draw_quad_offsets(jax.random.fold_in(arg_keys[7], 71), 0),
        "quad_weights": jnp.clip(jax.random.uniform(arg_keys[6], (2,), jnp.float32, 0.2, 0.8), 0.2, 0.8),
    }


gravity = 9.81
base_freq = 0.03
freq_ratio = 1.05
cell_size = 20.0
sub_step = 2.0
coupling = 0.01
coef_plus = 0.4096
coef_minus = 3.1605
coef_both = 2.589

def physics(radian_freq, water_depth, dir_count):
    square = (radian_freq * radian_freq)[None, :, None]
    column = water_depth[:, None, :]
    depth_ratio = square * column / gravity
    depth_wave = depth_ratio / jnp.sqrt(jnp.tanh(depth_ratio))
    group_speed = radian_freq[None, :, None] * column / depth_wave * (0.5 + depth_wave / jnp.sinh(2.0 * depth_wave))
    orbit_weight = square / jnp.sinh(depth_wave) ** 2 * (radian_freq * (freq_ratio - 1.0))[None, :, None] * (2.0 * math.pi / dir_count)
    return (group_speed, orbit_weight)

def angles_of(dir_count):
    angles = (jnp.arange(dir_count, dtype=jnp.float32) + 0.5) * (2.0 * math.pi / dir_count)
    return (jnp.cos(angles), jnp.sin(angles))

def shifted(doubled, freq_off, dir_off, count):
    dir_count = doubled.shape[2] // 2
    starts = (jnp.zeros((), jnp.int32), (freq_off + FH).astype(jnp.int32), (dir_off % dir_count).astype(jnp.int32), jnp.zeros((), jnp.int32))
    return lax.dynamic_slice(doubled, starts, (doubled.shape[0], count, dir_count, doubled.shape[3]))

def interaction(extended, masked, quad_offsets, quad_weights):
    count = masked.shape[1]
    doubled = jnp.concatenate([extended, extended], axis=2)
    up_bins, down_bins, up_turn, down_turn = (quad_offsets[0], quad_offsets[1], quad_offsets[2], quad_offsets[3])
    weight_up, weight_down = (quad_weights[0], quad_weights[1])
    upper = weight_up * shifted(doubled, up_bins, up_turn, count) + (1.0 - weight_up) * shifted(doubled, up_bins + 1, up_turn, count)
    lower = weight_down * shifted(doubled, -down_bins, -down_turn, count) + (1.0 - weight_down) * shifted(doubled, -down_bins - 1, -down_turn, count)
    return coupling * (masked * masked * (coef_plus * upper + coef_minus * lower) - coef_both * masked * upper * lower)

def redistribute(extended, transfer, quad_offsets, quad_weights):
    count = transfer.shape[1]
    doubled = jnp.concatenate([extended, extended], axis=2)
    up_bins, down_bins, up_turn, down_turn = (quad_offsets[0], quad_offsets[1], quad_offsets[2], quad_offsets[3])
    weight_up, weight_down = (quad_weights[0], quad_weights[1])
    gained = weight_up * shifted(doubled, -up_bins, -up_turn, count) + (1.0 - weight_up) * shifted(doubled, -up_bins - 1, -up_turn, count)
    gained = gained + weight_down * shifted(doubled, down_bins, down_turn, count) + (1.0 - weight_down) * shifted(doubled, down_bins + 1, down_turn, count)
    return gained - 2.0 * transfer

def east_west(east_flux, cosines):
    zeros = jnp.zeros_like(east_flux[..., :1])
    behind = jnp.concatenate([zeros, east_flux[..., :-1]], axis=-1)
    ahead = jnp.concatenate([east_flux[..., 1:], zeros], axis=-1)
    east_going = (cosines > 0.0).astype(jnp.float32)[None, None, :, None]
    return east_going * (east_flux - behind) + (1.0 - east_going) * (ahead - east_flux)

def reference(energy, water_depth, wet_mask, vegetation, canopy, quad_offsets, quad_weights):
    wet_field = wet_mask.astype(jnp.float32)
    veg_field = vegetation.astype(jnp.float32)
    masked = wet_field[:, None, None, :] * energy
    radian_freq = 2.0 * math.pi * base_freq * jnp.power(freq_ratio, jnp.arange(FREQS, dtype=jnp.float32))
    group_speed, orbit_weight = physics(radian_freq, water_depth, DIRS)
    orbital = jnp.sqrt(lax.optimization_barrier(jnp.sum(orbit_weight * lax.optimization_barrier(jnp.sum(energy, axis=2)), axis=1)))
    full_step = SUBSTEPS * sub_step
    damping = 1.0 + full_step * canopy * veg_field * orbital
    padding = ((0, 0), (FH, FH), (0, 0), (0, 0))
    blocks = NY // CY

    def source_block(items):
        block_masked, block_damp = items
        transfer = interaction(jnp.pad(block_masked, padding), block_masked, quad_offsets, quad_weights)
        change = redistribute(jnp.pad(transfer, padding), transfer, quad_offsets, quad_weights)
        return (block_masked + full_step * change) / block_damp[:, None, None, :] - block_masked
    increment = lax.map(source_block, (masked.reshape(blocks, CY, FREQS, DIRS, NX), damping.reshape(blocks, CY, NX)))
    increment = increment.reshape(NY, FREQS, DIRS, NX)
    cosines, sines = angles_of(DIRS)
    wet_four = wet_field[:, None, None, :]

    def move_one(items):
        spectrum, speed = items
        spectrum = spectrum[:, None]
        speed = speed[:, None]
        east_speed = speed[:, :, None, :] * cosines[None, None, :, None]
        north_speed = speed[:, :, None, :] * sines[None, None, :, None]
        north_going = (sines > 0.0).astype(jnp.float32)[None, None, :, None]
        for substep in range(SUBSTEPS):
            east_flux = east_speed * spectrum
            north_flux = north_speed * spectrum
            zeros = jnp.zeros_like(north_flux[:1])
            below = jnp.concatenate([zeros, north_flux[:-1]], axis=0)
            above = jnp.concatenate([north_flux[1:], zeros], axis=0)
            along = north_going * (north_flux - below) + (1.0 - north_going) * (above - north_flux)
            spectrum = wet_four * (spectrum - sub_step / cell_size * (east_west(east_flux, cosines) + along))
        return spectrum[:, 0]
    moved = lax.map(move_one, (jnp.moveaxis(masked, 1, 0), jnp.moveaxis(group_speed, 1, 0)))
    moved = jnp.moveaxis(moved, 0, 1)
    return (wet_four * (moved + increment), orbital)
```

```python
import math

import jax
import jax.numpy as jnp
from jax import lax
from jax.sharding import PartitionSpec as P

FH = 4
SUBSTEPS = 8


gravity = 9.81
base_freq = 0.03
freq_ratio = 1.05
cell_size = 20.0
sub_step = 2.0
coupling = 0.01
coef_plus = 0.4096
coef_minus = 3.1605
coef_both = 2.589


def from_neighbour(block, axis, distance):
    count = lax.axis_size(axis)
    pairs = [(i, i + distance) for i in range(count) if 0 <= i + distance < count]
    return lax.ppermute(block, axis, pairs)


def halo(block, axis, dim, width, side):
    size = block.shape[dim]
    parts = []
    distance = 1
    need = width
    while need > 0:
        take = min(size, need)
        if side < 0:
            piece = lax.slice_in_dim(block, size - take, size, axis=dim)
            parts.insert(0, from_neighbour(piece, axis, distance))
        else:
            piece = lax.slice_in_dim(block, 0, take, axis=dim)
            parts.append(from_neighbour(piece, axis, -distance))
        need -= take
        distance += 1
    return parts


def physics(radian_freq, water_depth, dir_count):
    square = (radian_freq * radian_freq)[None, :, None]
    column = water_depth[:, None, :]
    depth_ratio = square * column / gravity
    depth_wave = depth_ratio / jnp.sqrt(jnp.tanh(depth_ratio))
    group_speed = (
        radian_freq[None, :, None]
        * column
        / depth_wave
        * (0.5 + depth_wave / jnp.sinh(2.0 * depth_wave))
    )
    orbit_weight = (
        square
        / jnp.sinh(depth_wave) ** 2
        * (radian_freq * (freq_ratio - 1.0))[None, :, None]
        * (2.0 * math.pi / dir_count)
    )
    return (group_speed, orbit_weight)


def angles_of(dir_count):
    angles = (jnp.arange(dir_count, dtype=jnp.float32) + 0.5) * (2.0 * math.pi / dir_count)
    return (jnp.cos(angles), jnp.sin(angles))


def shifted(doubled, freq_start, dir_off, count):
    dir_count = doubled.shape[2] // 2
    starts = (
        jnp.zeros((), jnp.int32),
        freq_start,
        dir_off % dir_count,
        jnp.zeros((), jnp.int32),
    )
    return lax.dynamic_slice(
        doubled, starts, (doubled.shape[0], count, dir_count, doubled.shape[3])
    )


def source_change(extended, quad_offsets, quad_weights, count):
    up_bins, down_bins, up_turn, down_turn = (
        quad_offsets[0],
        quad_offsets[1],
        quad_offsets[2],
        quad_offsets[3],
    )
    weight_up, weight_down = (quad_weights[0], quad_weights[1])
    wide = count + 2 * FH
    doubled = jnp.concatenate([extended, extended], axis=2)
    centre = lax.slice_in_dim(extended, FH, FH + wide, axis=1)
    upper = weight_up * shifted(doubled, FH + up_bins, up_turn, wide) + (
        1.0 - weight_up
    ) * shifted(doubled, FH + up_bins + 1, up_turn, wide)
    lower = weight_down * shifted(doubled, FH - down_bins, -down_turn, wide) + (
        1.0 - weight_down
    ) * shifted(doubled, FH - down_bins - 1, -down_turn, wide)
    transfer = coupling * (
        centre * centre * (coef_plus * upper + coef_minus * lower)
        - coef_both * centre * upper * lower
    )
    spread = jnp.concatenate([transfer, transfer], axis=2)
    gained = weight_up * shifted(spread, FH - up_bins, -up_turn, count) + (
        1.0 - weight_up
    ) * shifted(spread, FH - up_bins - 1, -up_turn, count)
    gained = (
        gained
        + weight_down * shifted(spread, FH + down_bins, down_turn, count)
        + (1.0 - weight_down) * shifted(spread, FH + down_bins + 1, down_turn, count)
    )
    own = lax.slice_in_dim(transfer, FH, FH + count, axis=1)
    return gained - 2.0 * own


def east_west(east_flux, cosines):
    zeros = jnp.zeros_like(east_flux[..., :1])
    behind = jnp.concatenate([zeros, east_flux[..., :-1]], axis=-1)
    ahead = jnp.concatenate([east_flux[..., 1:], zeros], axis=-1)
    east_going = (cosines > 0.0)[None, None, :, None]
    return jnp.where(east_going, east_flux - behind, ahead - east_flux)


def propagate(spectrum, speed, wet, cosines, sines, northward):
    step_ratio = sub_step / cell_size
    east_speed = speed[:, :, None, :] * cosines[None, None, :, None]
    north_speed = speed[:, :, None, :] * sines[None, None, :, None]
    rows = spectrum.shape[0]
    for substep in range(SUBSTEPS):
        lo, hi = (substep, rows) if northward else (0, rows - substep)
        east_flux = east_speed[lo:hi] * spectrum
        north_flux = north_speed[lo:hi] * spectrum
        along = north_flux[1:] - north_flux[:-1]
        across = east_west(east_flux, cosines)
        if northward:
            spectrum = wet[lo + 1 : hi, None, None, :] * (
                spectrum[1:] - step_ratio * (across[1:] + along)
            )
        else:
            spectrum = wet[lo : hi - 1, None, None, :] * (
                spectrum[:-1] - step_ratio * (across[:-1] + along)
            )
    return spectrum


def body(energy, water_depth, wet_mask, vegetation, canopy, quad_offsets, quad_weights):
    tile_rows, freq_count, dir_count, tile_cols = energy.shape
    wet_field = wet_mask.astype(jnp.float32)
    veg_field = vegetation.astype(jnp.float32)
    wet_four = wet_field[:, None, None, :]
    masked = wet_four * energy
    first_bin = lax.axis_index("freq") * freq_count
    bin_index = (first_bin + jnp.arange(freq_count, dtype=jnp.int32)).astype(jnp.float32)
    radian_freq = 2.0 * math.pi * base_freq * jnp.power(freq_ratio, bin_index)
    half = dir_count // 2
    cosines, sines = angles_of(dir_count)

    fields = jnp.zeros((tile_rows, 1, half, tile_cols), jnp.float32)
    fields = fields.at[:, 0, 0, :].set(wet_field).at[:, 0, 1, :].set(water_depth)
    north_msg = jnp.concatenate([masked[:, :, :half], fields], axis=1)
    south_msg = jnp.concatenate([masked[:, :, half:], fields], axis=1)
    below = halo(north_msg, "geo", 0, SUBSTEPS, -1)
    above = halo(south_msg, "geo", 0, SUBSTEPS, +1)

    low_bins = halo(masked, "freq", 1, 2 * FH, -1)
    high_bins = halo(masked, "freq", 1, 2 * FH, +1)

    group_speed, orbit_weight = physics(radian_freq, water_depth, dir_count)
    partial_value = jnp.sum(orbit_weight * jnp.sum(energy, axis=2), axis=1)
    orbital = jnp.sqrt(lax.psum(partial_value, "freq"))
    full_step = SUBSTEPS * sub_step
    damping = 1.0 + full_step * canopy * veg_field * orbital

    extended = jnp.concatenate(low_bins + [masked] + high_bins, axis=1)
    change = source_change(extended, quad_offsets, quad_weights, freq_count)
    increment = (masked + full_step * change) / damping[:, None, None, :] - masked

    geo_index = lax.axis_index("geo")
    geo_count = lax.axis_size("geo")

    def unpack(parts, offsets, own, own_speed, own_wet):
        spectra, speeds, wets = [], [], []
        for part, offset in zip(parts, offsets):
            valid = (geo_index + offset >= 0) & (geo_index + offset < geo_count)
            depth = jnp.where(valid, part[:, freq_count, 1, :], 1.0)
            spectra.append(part[:, :freq_count])
            wets.append(part[:, freq_count, 0, :])
            speeds.append(physics(radian_freq, depth, dir_count)[0])
        return spectra, speeds, wets

    n_off = [-(len(below) - k) for k in range(len(below))]
    b_spec, b_speed, b_wet = unpack(below, n_off, None, None, None)
    north = propagate(
        jnp.concatenate(b_spec + [masked[:, :, :half]], axis=0),
        jnp.concatenate(b_speed + [group_speed], axis=0),
        jnp.concatenate(b_wet + [wet_field], axis=0),
        cosines[:half],
        sines[:half],
        True,
    )
    s_off = [k + 1 for k in range(len(above))]
    a_spec, a_speed, a_wet = unpack(above, s_off, None, None, None)
    south = propagate(
        jnp.concatenate([masked[:, :, half:]] + a_spec, axis=0),
        jnp.concatenate([group_speed] + a_speed, axis=0),
        jnp.concatenate([wet_field] + a_wet, axis=0),
        cosines[half:],
        sines[half:],
        False,
    )
    moved = jnp.concatenate([north, south], axis=2)
    return (wet_four * (moved + increment), orbital)


def solution(mesh):
    placed = (
        P("geo", "freq", None, None),
        P("geo", None),
        P("geo", None),
        P("geo", None),
        P("geo", None),
        P(),
        P(),
    )
    return jax.shard_map(
        body,
        mesh=mesh,
        in_specs=placed,
        out_specs=(P("geo", "freq", None, None), P("geo", None)),
        check_vma=False,
    )
```

```python
import math

import jax
import jax.numpy as jnp
from jax import lax
from jax.sharding import PartitionSpec as P

FH = 4
SUBSTEPS = 8


gravity = 9.81
base_freq = 0.03
freq_ratio = 1.05
cell_size = 20.0
sub_step = 2.0
coupling = 0.01
coef_plus = 0.4096
coef_minus = 3.1605
coef_both = 2.589


def from_neighbour(block, axis, distance):
    count = lax.axis_size(axis)
    pairs = [(i, i + distance) for i in range(count) if 0 <= i + distance < count]
    return lax.ppermute(block, axis, pairs)


def halo(block, axis, dim, width, side):
    size = block.shape[dim]
    parts = []
    distance = 1
    need = width
    while need > 0:
        take = min(size, need)
        if side < 0:
            piece = lax.slice_in_dim(block, size - take, size, axis=dim)
            parts.insert(0, from_neighbour(piece, axis, distance))
        else:
            piece = lax.slice_in_dim(block, 0, take, axis=dim)
            parts.append(from_neighbour(piece, axis, -distance))
        need -= take
        distance += 1
    return parts


def butterfly_sum(value, axis):
    count = lax.axis_size(axis)
    assert count & (count - 1) == 0
    step = 1
    while step < count:
        value = value + lax.ppermute(value, axis, [(i, i ^ step) for i in range(count)])
        step *= 2
    return value


def physics(radian_freq, water_depth, dir_count):
    square = (radian_freq * radian_freq)[None, :, None]
    column = water_depth[:, None, :]
    depth_ratio = square * column / gravity
    depth_wave = depth_ratio / jnp.sqrt(jnp.tanh(depth_ratio))
    group_speed = (
        radian_freq[None, :, None]
        * column
        / depth_wave
        * (0.5 + depth_wave / jnp.sinh(2.0 * depth_wave))
    )
    orbit_weight = (
        square
        / jnp.sinh(depth_wave) ** 2
        * (radian_freq * (freq_ratio - 1.0))[None, :, None]
        * (2.0 * math.pi / dir_count)
    )
    return (group_speed, orbit_weight)


def angles_of(dir_count):
    angles = (jnp.arange(dir_count, dtype=jnp.float32) + 0.5) * (2.0 * math.pi / dir_count)
    return (jnp.cos(angles), jnp.sin(angles))


def shifted(doubled, freq_start, dir_off, count):
    dir_count = doubled.shape[2] // 2
    starts = (
        jnp.zeros((), jnp.int32),
        freq_start,
        dir_off % dir_count,
        jnp.zeros((), jnp.int32),
    )
    return lax.dynamic_slice(
        doubled, starts, (doubled.shape[0], count, dir_count, doubled.shape[3])
    )


def source_change(extended, quad_offsets, quad_weights, count):
    up_bins, down_bins, up_turn, down_turn = (
        quad_offsets[0],
        quad_offsets[1],
        quad_offsets[2],
        quad_offsets[3],
    )
    weight_up, weight_down = (quad_weights[0], quad_weights[1])
    wide = count + 2 * FH
    doubled = jnp.concatenate([extended, extended], axis=2)
    centre = lax.slice_in_dim(extended, FH, FH + wide, axis=1)
    upper = weight_up * shifted(doubled, FH + up_bins, up_turn, wide) + (
        1.0 - weight_up
    ) * shifted(doubled, FH + up_bins + 1, up_turn, wide)
    lower = weight_down * shifted(doubled, FH - down_bins, -down_turn, wide) + (
        1.0 - weight_down
    ) * shifted(doubled, FH - down_bins - 1, -down_turn, wide)
    transfer = coupling * (
        centre * centre * (coef_plus * upper + coef_minus * lower)
        - coef_both * centre * upper * lower
    )
    spread = jnp.concatenate([transfer, transfer], axis=2)
    gained = weight_up * shifted(spread, FH - up_bins, -up_turn, count) + (
        1.0 - weight_up
    ) * shifted(spread, FH - up_bins - 1, -up_turn, count)
    gained = (
        gained
        + weight_down * shifted(spread, FH + down_bins, down_turn, count)
        + (1.0 - weight_down) * shifted(spread, FH + down_bins + 1, down_turn, count)
    )
    own = lax.slice_in_dim(transfer, FH, FH + count, axis=1)
    return gained - 2.0 * own


def east_west(east_flux, cosines):
    zeros = jnp.zeros_like(east_flux[..., :1])
    behind = jnp.concatenate([zeros, east_flux[..., :-1]], axis=-1)
    ahead = jnp.concatenate([east_flux[..., 1:], zeros], axis=-1)
    east_going = (cosines > 0.0)[None, None, :, None]
    return jnp.where(east_going, east_flux - behind, ahead - east_flux)


def propagate(spectrum, speed, wet, cosines, sines, northward):
    step_ratio = sub_step / cell_size
    east_speed = speed[:, :, None, :] * cosines[None, None, :, None]
    north_speed = speed[:, :, None, :] * sines[None, None, :, None]
    rows = spectrum.shape[0]
    for substep in range(SUBSTEPS):
        lo, hi = (substep, rows) if northward else (0, rows - substep)
        east_flux = east_speed[lo:hi] * spectrum
        north_flux = north_speed[lo:hi] * spectrum
        along = north_flux[1:] - north_flux[:-1]
        across = east_west(east_flux, cosines)
        if northward:
            spectrum = wet[lo + 1 : hi, None, None, :] * (
                spectrum[1:] - step_ratio * (across[1:] + along)
            )
        else:
            spectrum = wet[lo : hi - 1, None, None, :] * (
                spectrum[:-1] - step_ratio * (across[:-1] + along)
            )
    return spectrum


def body(energy, water_depth, wet_mask, vegetation, canopy, quad_offsets, quad_weights):
    tile_rows, freq_count, dir_count, tile_cols = energy.shape
    wet_field = wet_mask.astype(jnp.float32)
    veg_field = vegetation.astype(jnp.float32)
    wet_four = wet_field[:, None, None, :]
    masked = wet_four * energy
    first_bin = lax.axis_index("freq") * freq_count
    bin_index = (first_bin + jnp.arange(freq_count, dtype=jnp.int32)).astype(jnp.float32)
    radian_freq = 2.0 * math.pi * base_freq * jnp.power(freq_ratio, bin_index)
    half = dir_count // 2
    cosines, sines = angles_of(dir_count)

    fields = jnp.zeros((tile_rows, 1, half, tile_cols), jnp.float32)
    fields = fields.at[:, 0, 0, :].set(wet_field).at[:, 0, 1, :].set(water_depth)
    north_msg = jnp.concatenate([masked[:, :, :half], fields], axis=1)
    south_msg = jnp.concatenate([masked[:, :, half:], fields], axis=1)
    below = halo(north_msg, "geo", 0, SUBSTEPS, -1)
    above = halo(south_msg, "geo", 0, SUBSTEPS, +1)

    low_bins = halo(masked, "freq", 1, 2 * FH, -1)
    high_bins = halo(masked, "freq", 1, 2 * FH, +1)

    group_speed, orbit_weight = physics(radian_freq, water_depth, dir_count)
    partial_value = jnp.sum(orbit_weight * jnp.sum(energy, axis=2), axis=1)
    orbital = jnp.sqrt(butterfly_sum(partial_value, "freq"))
    full_step = SUBSTEPS * sub_step
    damping = 1.0 + full_step * canopy * veg_field * orbital

    extended = jnp.concatenate(low_bins + [masked] + high_bins, axis=1)
    change = source_change(extended, quad_offsets, quad_weights, freq_count)
    increment = (masked + full_step * change) / damping[:, None, None, :] - masked

    geo_index = lax.axis_index("geo")
    geo_count = lax.axis_size("geo")

    def unpack(parts, offsets):
        spectra, speeds, wets = [], [], []
        for part, offset in zip(parts, offsets):
            valid = (geo_index + offset >= 0) & (geo_index + offset < geo_count)
            depth = jnp.where(valid, part[:, freq_count, 1, :], 1.0)
            spectra.append(part[:, :freq_count])
            wets.append(part[:, freq_count, 0, :])
            speeds.append(physics(radian_freq, depth, dir_count)[0])
        return spectra, speeds, wets

    n_off = [-(len(below) - k) for k in range(len(below))]
    b_spec, b_speed, b_wet = unpack(below, n_off)
    north = propagate(
        jnp.concatenate(b_spec + [masked[:, :, :half]], axis=0),
        jnp.concatenate(b_speed + [group_speed], axis=0),
        jnp.concatenate(b_wet + [wet_field], axis=0),
        cosines[:half],
        sines[:half],
        True,
    )
    s_off = [k + 1 for k in range(len(above))]
    a_spec, a_speed, a_wet = unpack(above, s_off)
    south = propagate(
        jnp.concatenate([masked[:, :, half:]] + a_spec, axis=0),
        jnp.concatenate([group_speed] + a_speed, axis=0),
        jnp.concatenate([wet_field] + a_wet, axis=0),
        cosines[half:],
        sines[half:],
        False,
    )
    moved = jnp.concatenate([north, south], axis=2)
    return (wet_four * (moved + increment), orbital)


def solution(mesh):
    placed = (
        P("geo", "freq", None, None),
        P("geo", None),
        P("geo", None),
        P("geo", None),
        P("geo", None),
        P(),
        P(),
    )
    return jax.shard_map(
        body,
        mesh=mesh,
        in_specs=placed,
        out_specs=(P("geo", "freq", None, None), P("geo", None)),
        check_vma=False,
    )
```

```python
import math

import jax
import jax.numpy as jnp
from jax import lax
from jax.sharding import PartitionSpec as P

FH = 4
SUBSTEPS = 8


gravity = 9.81
base_freq = 0.03
freq_ratio = 1.05
cell_size = 20.0
sub_step = 2.0
coupling = 0.01
coef_plus = 0.4096
coef_minus = 3.1605
coef_both = 2.589


def from_neighbour(block, axis, distance, cyclic=False):
    count = lax.axis_size(axis)
    if cyclic:
        pairs = [(i, (i + distance) % count) for i in range(count)]
    else:
        pairs = [(i, i + distance) for i in range(count) if 0 <= i + distance < count]
    return lax.ppermute(block, axis, pairs)


def halo(block, axis, dim, width, side, cyclic=False):
    size = block.shape[dim]
    parts = []
    distance = 1
    need = width
    while need > 0:
        take = min(size, need)
        if side < 0:
            piece = lax.slice_in_dim(block, size - take, size, axis=dim)
            parts.insert(0, from_neighbour(piece, axis, distance, cyclic))
        else:
            piece = lax.slice_in_dim(block, 0, take, axis=dim)
            parts.append(from_neighbour(piece, axis, -distance, cyclic))
        need -= take
        distance += 1
    return parts


def butterfly_sum(value, axis):
    count = lax.axis_size(axis)
    assert count & (count - 1) == 0
    step = 1
    while step < count:
        value = value + lax.ppermute(value, axis, [(i, i ^ step) for i in range(count)])
        step *= 2
    return value


def gathered_sum(known, index, count, value):
    reach = max(known)
    if count > 2 * (2 * reach + 1) - 2 or count % 2:
        return butterfly_sum(value, "freq")
    far = count // 2
    ordered = jnp.stack([known[o] for o in range(-reach, reach + 1)])
    more = from_neighbour(ordered, "freq", far, True)
    table = []
    for rel in range(count):
        off = rel if rel <= reach else rel - count
        if -reach <= off <= reach:
            table.append(known[off])
        else:
            table.append(more[rel - far + reach])
    table = jnp.stack(table)
    table = jnp.concatenate([table, table], axis=0)
    start = (count - index) % count
    glob = lax.dynamic_slice_in_dim(table, start, count, axis=0)
    while glob.shape[0] > 1:
        glob = glob[0::2] + glob[1::2]
    return glob[0]


def physics(radian_freq, water_depth, dir_count):
    square = (radian_freq * radian_freq)[None, :, None]
    column = water_depth[:, None, :]
    depth_ratio = square * column / gravity
    depth_wave = depth_ratio / jnp.sqrt(jnp.tanh(depth_ratio))
    group_speed = (
        radian_freq[None, :, None]
        * column
        / depth_wave
        * (0.5 + depth_wave / jnp.sinh(2.0 * depth_wave))
    )
    orbit_weight = (
        square
        / jnp.sinh(depth_wave) ** 2
        * (radian_freq * (freq_ratio - 1.0))[None, :, None]
        * (2.0 * math.pi / dir_count)
    )
    return (group_speed, orbit_weight)


def angles_of(dir_count):
    angles = (jnp.arange(dir_count, dtype=jnp.float32) + 0.5) * (2.0 * math.pi / dir_count)
    return (jnp.cos(angles), jnp.sin(angles))


def shifted(doubled, freq_start, dir_off, count):
    dir_count = doubled.shape[2] // 2
    starts = (
        jnp.zeros((), jnp.int32),
        freq_start,
        dir_off % dir_count,
        jnp.zeros((), jnp.int32),
    )
    return lax.dynamic_slice(
        doubled, starts, (doubled.shape[0], count, dir_count, doubled.shape[3])
    )


def source_change(extended, quad_offsets, quad_weights, count):
    up_bins, down_bins, up_turn, down_turn = (
        quad_offsets[0],
        quad_offsets[1],
        quad_offsets[2],
        quad_offsets[3],
    )
    weight_up, weight_down = (quad_weights[0], quad_weights[1])
    wide = count + 2 * FH
    doubled = jnp.concatenate([extended, extended], axis=2)
    centre = lax.slice_in_dim(extended, FH, FH + wide, axis=1)
    upper = weight_up * shifted(doubled, FH + up_bins, up_turn, wide) + (
        1.0 - weight_up
    ) * shifted(doubled, FH + up_bins + 1, up_turn, wide)
    lower = weight_down * shifted(doubled, FH - down_bins, -down_turn, wide) + (
        1.0 - weight_down
    ) * shifted(doubled, FH - down_bins - 1, -down_turn, wide)
    transfer = coupling * (
        centre * centre * (coef_plus * upper + coef_minus * lower)
        - coef_both * centre * upper * lower
    )
    spread = jnp.concatenate([transfer, transfer], axis=2)
    gained = weight_up * shifted(spread, FH - up_bins, -up_turn, count) + (
        1.0 - weight_up
    ) * shifted(spread, FH - up_bins - 1, -up_turn, count)
    gained = (
        gained
        + weight_down * shifted(spread, FH + down_bins, down_turn, count)
        + (1.0 - weight_down) * shifted(spread, FH + down_bins + 1, down_turn, count)
    )
    own = lax.slice_in_dim(transfer, FH, FH + count, axis=1)
    return gained - 2.0 * own


def east_west(east_flux, cosines):
    zeros = jnp.zeros_like(east_flux[..., :1])
    behind = jnp.concatenate([zeros, east_flux[..., :-1]], axis=-1)
    ahead = jnp.concatenate([east_flux[..., 1:], zeros], axis=-1)
    east_going = (cosines > 0.0)[None, None, :, None]
    return jnp.where(east_going, east_flux - behind, ahead - east_flux)


def propagate(spectrum, speed, wet, cosines, sines, northward):
    step_ratio = sub_step / cell_size
    east_speed = speed[:, :, None, :] * cosines[None, None, :, None]
    north_speed = speed[:, :, None, :] * sines[None, None, :, None]
    rows = spectrum.shape[0]
    for substep in range(SUBSTEPS):
        lo, hi = (substep, rows) if northward else (0, rows - substep)
        east_flux = east_speed[lo:hi] * spectrum
        north_flux = north_speed[lo:hi] * spectrum
        along = north_flux[1:] - north_flux[:-1]
        across = east_west(east_flux, cosines)
        if northward:
            spectrum = wet[lo + 1 : hi, None, None, :] * (
                spectrum[1:] - step_ratio * (across[1:] + along)
            )
        else:
            spectrum = wet[lo : hi - 1, None, None, :] * (
                spectrum[:-1] - step_ratio * (across[:-1] + along)
            )
    return spectrum


def body(energy, water_depth, wet_mask, vegetation, canopy, quad_offsets, quad_weights):
    tile_rows, freq_count, dir_count, tile_cols = energy.shape
    wet_field = wet_mask.astype(jnp.float32)
    veg_field = vegetation.astype(jnp.float32)
    wet_four = wet_field[:, None, None, :]
    masked = wet_four * energy
    first_bin = lax.axis_index("freq") * freq_count
    bin_index = (first_bin + jnp.arange(freq_count, dtype=jnp.int32)).astype(jnp.float32)
    radian_freq = 2.0 * math.pi * base_freq * jnp.power(freq_ratio, bin_index)
    half = dir_count // 2
    cosines, sines = angles_of(dir_count)

    fields = jnp.zeros((tile_rows, 1, half, tile_cols), jnp.float32)
    fields = fields.at[:, 0, 0, :].set(wet_field).at[:, 0, 1, :].set(water_depth)
    north_msg = jnp.concatenate([masked[:, :, :half], fields], axis=1)
    south_msg = jnp.concatenate([masked[:, :, half:], fields], axis=1)
    below = halo(north_msg, "geo", 0, SUBSTEPS, -1)
    above = halo(south_msg, "geo", 0, SUBSTEPS, +1)

    group_speed, orbit_weight = physics(radian_freq, water_depth, dir_count)
    partial_value = jnp.sum(orbit_weight * jnp.sum(energy, axis=2), axis=1)

    freq_index = lax.axis_index("freq")
    freq_total = lax.axis_size("freq")
    slot = jnp.zeros((tile_rows, 1, dir_count, tile_cols), jnp.float32)
    slot = slot.at[:, 0, 0, :].set(partial_value)

    def tagged_halo(side):
        pieces = []
        distance = 1
        need = 2 * FH
        while need > 0:
            take = min(freq_count, need)
            lo = freq_count - take if side < 0 else 0
            piece = jnp.concatenate(
                [lax.slice_in_dim(masked, lo, lo + take, axis=1), slot], axis=1
            )
            got = from_neighbour(piece, "freq", -side * distance, True)
            source = freq_index + side * distance
            inside = (source >= 0) & (source < freq_total)
            pieces.append(
                (distance * side, jnp.where(inside, got[:, :take], 0.0), got[:, take, 0, :])
            )
            need -= take
            distance += 1
        return pieces

    low = tagged_halo(-1)
    high = tagged_halo(+1)
    low_bins = [p[1] for p in reversed(low)]
    high_bins = [p[1] for p in high]
    known = {0: partial_value}
    for offset, _, value in low + high:
        known[offset] = value
    orbital = jnp.sqrt(gathered_sum(known, freq_index, freq_total, partial_value))
    full_step = SUBSTEPS * sub_step
    damping = 1.0 + full_step * canopy * veg_field * orbital

    extended = jnp.concatenate(low_bins + [masked] + high_bins, axis=1)
    change = source_change(extended, quad_offsets, quad_weights, freq_count)
    increment = (masked + full_step * change) / damping[:, None, None, :] - masked

    geo_index = lax.axis_index("geo")
    geo_count = lax.axis_size("geo")

    def unpack(parts, offsets):
        spectra, speeds, wets = [], [], []
        for part, offset in zip(parts, offsets):
            valid = (geo_index + offset >= 0) & (geo_index + offset < geo_count)
            depth = jnp.where(valid, part[:, freq_count, 1, :], 1.0)
            spectra.append(part[:, :freq_count])
            wets.append(part[:, freq_count, 0, :])
            speeds.append(physics(radian_freq, depth, dir_count)[0])
        return spectra, speeds, wets

    n_off = [-(len(below) - k) for k in range(len(below))]
    b_spec, b_speed, b_wet = unpack(below, n_off)
    north = propagate(
        jnp.concatenate(b_spec + [masked[:, :, :half]], axis=0),
        jnp.concatenate(b_speed + [group_speed], axis=0),
        jnp.concatenate(b_wet + [wet_field], axis=0),
        cosines[:half],
        sines[:half],
        True,
    )
    s_off = [k + 1 for k in range(len(above))]
    a_spec, a_speed, a_wet = unpack(above, s_off)
    south = propagate(
        jnp.concatenate([masked[:, :, half:]] + a_spec, axis=0),
        jnp.concatenate([group_speed] + a_speed, axis=0),
        jnp.concatenate([wet_field] + a_wet, axis=0),
        cosines[half:],
        sines[half:],
        False,
    )
    moved = jnp.concatenate([north, south], axis=2)
    return (wet_four * (moved + increment), orbital)


def solution(mesh):
    placed = (
        P("geo", "freq", None, None),
        P("geo", None),
        P("geo", None),
        P("geo", None),
        P("geo", None),
        P(),
        P(),
    )
    return jax.shard_map(
        body,
        mesh=mesh,
        in_specs=placed,
        out_specs=(P("geo", "freq", None, None), P("geo", None)),
        check_vma=False,
    )
```

```python
import functools
import math

import jax
import jax.numpy as jnp
from jax import lax
from jax.experimental import pallas as pl
from jax.experimental.pallas import tpu as pltpu
from jax.sharding import PartitionSpec as P

INTERPRET = False

FH = 4
SUBSTEPS = 8


gravity = 9.81
base_freq = 0.03
freq_ratio = 1.05
cell_size = 20.0
sub_step = 2.0
coupling = 0.01
coef_plus = 0.4096
coef_minus = 3.1605
coef_both = 2.589


def from_neighbour(block, axis, distance, cyclic=False):
    count = lax.axis_size(axis)
    if cyclic:
        pairs = [(i, (i + distance) % count) for i in range(count)]
    else:
        pairs = [(i, i + distance) for i in range(count) if 0 <= i + distance < count]
    return lax.ppermute(block, axis, pairs)


def halo(block, axis, dim, width, side, cyclic=False):
    size = block.shape[dim]
    parts = []
    distance = 1
    need = width
    while need > 0:
        take = min(size, need)
        if side < 0:
            piece = lax.slice_in_dim(block, size - take, size, axis=dim)
            parts.insert(0, from_neighbour(piece, axis, distance, cyclic))
        else:
            piece = lax.slice_in_dim(block, 0, take, axis=dim)
            parts.append(from_neighbour(piece, axis, -distance, cyclic))
        need -= take
        distance += 1
    return parts


def butterfly_sum(value, axis):
    count = lax.axis_size(axis)
    assert count & (count - 1) == 0
    step = 1
    while step < count:
        value = value + lax.ppermute(value, axis, [(i, i ^ step) for i in range(count)])
        step *= 2
    return value


def gathered_sum(known, index, count, value):
    reach = max(known)
    if count > 2 * (2 * reach + 1) - 2 or count % 2:
        return butterfly_sum(value, "freq")
    far = count // 2
    ordered = jnp.stack([known[o] for o in range(-reach, reach + 1)])
    more = from_neighbour(ordered, "freq", far, True)
    table = []
    for rel in range(count):
        off = rel if rel <= reach else rel - count
        if -reach <= off <= reach:
            table.append(known[off])
        else:
            table.append(more[rel - far + reach])
    table = jnp.stack(table)
    table = jnp.concatenate([table, table], axis=0)
    start = (count - index) % count
    glob = lax.dynamic_slice_in_dim(table, start, count, axis=0)
    while glob.shape[0] > 1:
        glob = glob[0::2] + glob[1::2]
    return glob[0]


def physics(radian_freq, water_depth, dir_count):
    square = (radian_freq * radian_freq)[None, :, None]
    column = water_depth[:, None, :]
    depth_ratio = square * column / gravity
    depth_wave = depth_ratio / jnp.sqrt(jnp.tanh(depth_ratio))
    group_speed = (
        radian_freq[None, :, None]
        * column
        / depth_wave
        * (0.5 + depth_wave / jnp.sinh(2.0 * depth_wave))
    )
    orbit_weight = (
        square
        / jnp.sinh(depth_wave) ** 2
        * (radian_freq * (freq_ratio - 1.0))[None, :, None]
        * (2.0 * math.pi / dir_count)
    )
    return (group_speed, orbit_weight)


def angles_of(dir_count):
    angles = (jnp.arange(dir_count, dtype=jnp.float32) + 0.5) * (2.0 * math.pi / dir_count)
    return (jnp.cos(angles), jnp.sin(angles))


def shifted(doubled, freq_start, dir_off, count):
    dir_count = doubled.shape[2] // 2
    starts = (
        jnp.zeros((), jnp.int32),
        freq_start,
        dir_off % dir_count,
        jnp.zeros((), jnp.int32),
    )
    return lax.dynamic_slice(
        doubled, starts, (doubled.shape[0], count, dir_count, doubled.shape[3])
    )


def source_change(extended, quad_offsets, quad_weights, count):
    up_bins, down_bins, up_turn, down_turn = (
        quad_offsets[0],
        quad_offsets[1],
        quad_offsets[2],
        quad_offsets[3],
    )
    weight_up, weight_down = (quad_weights[0], quad_weights[1])
    wide = count + 2 * FH
    doubled = jnp.concatenate([extended, extended], axis=2)
    centre = lax.slice_in_dim(extended, FH, FH + wide, axis=1)
    upper = weight_up * shifted(doubled, FH + up_bins, up_turn, wide) + (
        1.0 - weight_up
    ) * shifted(doubled, FH + up_bins + 1, up_turn, wide)
    lower = weight_down * shifted(doubled, FH - down_bins, -down_turn, wide) + (
        1.0 - weight_down
    ) * shifted(doubled, FH - down_bins - 1, -down_turn, wide)
    transfer = coupling * (
        centre * centre * (coef_plus * upper + coef_minus * lower)
        - coef_both * centre * upper * lower
    )
    spread = jnp.concatenate([transfer, transfer], axis=2)
    gained = weight_up * shifted(spread, FH - up_bins, -up_turn, count) + (
        1.0 - weight_up
    ) * shifted(spread, FH - up_bins - 1, -up_turn, count)
    gained = (
        gained
        + weight_down * shifted(spread, FH + down_bins, down_turn, count)
        + (1.0 - weight_down) * shifted(spread, FH + down_bins + 1, down_turn, count)
    )
    own = lax.slice_in_dim(transfer, FH, FH + count, axis=1)
    return gained - 2.0 * own


def east_west(east_flux, cosines):
    zeros = jnp.zeros_like(east_flux[..., :1])
    behind = jnp.concatenate([zeros, east_flux[..., :-1]], axis=-1)
    ahead = jnp.concatenate([east_flux[..., 1:], zeros], axis=-1)
    east_going = (cosines > 0.0)[None, None, :, None]
    return jnp.where(east_going, east_flux - behind, ahead - east_flux)


def propagate_kernel(p_ref, ex_ref, ny_ref, wet_ref, east_ref, o_ref, *, northward):
    step_ratio = sub_step / cell_size
    spectrum = p_ref[:, 0]
    east_speed = ex_ref[:, 0]
    north_speed = ny_ref[:, 0]
    wet = wet_ref[...]
    east_going = east_ref[...] > 0.0
    rows, _, cols = spectrum.shape
    col = lax.broadcasted_iota(jnp.int32, spectrum.shape[1:], 1)
    for substep in range(SUBSTEPS):
        lo, hi = (substep, rows) if northward else (0, rows - substep)
        east_flux = east_speed[lo:hi] * spectrum
        north_flux = north_speed[lo:hi] * spectrum
        behind = jnp.where(col == 0, 0.0, pltpu.roll(east_flux, 1, 2))
        ahead = jnp.where(col == cols - 1, 0.0, pltpu.roll(east_flux, cols - 1, 2))
        across = jnp.where(east_going, east_flux - behind, ahead - east_flux)
        along = north_flux[1:] - north_flux[:-1]
        if northward:
            spectrum = wet[lo + 1 : hi, None, :] * (
                spectrum[1:] - step_ratio * (across[1:] + along)
            )
        else:
            spectrum = wet[lo : hi - 1, None, :] * (
                spectrum[:-1] - step_ratio * (across[:-1] + along)
            )
    o_ref[:, 0] = spectrum


def propagate(spectrum, speed, wet, cosines, sines, northward):
    rows, freq_count, dirs, cols = spectrum.shape
    out_rows = rows - SUBSTEPS
    east_speed = speed[:, :, None, :] * cosines[None, None, :, None]
    north_speed = speed[:, :, None, :] * sines[None, None, :, None]
    east_going = jnp.broadcast_to((cosines > 0.0).astype(jnp.float32)[:, None], (dirs, cols))
    block = pl.BlockSpec((rows, 1, dirs, cols), lambda b: (0, b, 0, 0))
    whole = lambda shape: pl.BlockSpec(shape, lambda b: (0, 0))
    return pl.pallas_call(
        functools.partial(propagate_kernel, northward=northward),
        out_shape=jax.ShapeDtypeStruct((out_rows, freq_count, dirs, cols), jnp.float32),
        grid=(freq_count,),
        in_specs=[block, block, block, whole((rows, cols)), whole((dirs, cols))],
        out_specs=pl.BlockSpec((out_rows, 1, dirs, cols), lambda b: (0, b, 0, 0)),
        interpret=INTERPRET,
    )(spectrum, east_speed, north_speed, wet, east_going)


def body(energy, water_depth, wet_mask, vegetation, canopy, quad_offsets, quad_weights):
    tile_rows, freq_count, dir_count, tile_cols = energy.shape
    wet_field = wet_mask.astype(jnp.float32)
    veg_field = vegetation.astype(jnp.float32)
    wet_four = wet_field[:, None, None, :]
    masked = wet_four * energy
    first_bin = lax.axis_index("freq") * freq_count
    bin_index = (first_bin + jnp.arange(freq_count, dtype=jnp.int32)).astype(jnp.float32)
    radian_freq = 2.0 * math.pi * base_freq * jnp.power(freq_ratio, bin_index)
    half = dir_count // 2
    cosines, sines = angles_of(dir_count)

    fields = jnp.zeros((tile_rows, 1, half, tile_cols), jnp.float32)
    fields = fields.at[:, 0, 0, :].set(wet_field).at[:, 0, 1, :].set(water_depth)
    north_msg = jnp.concatenate([masked[:, :, :half], fields], axis=1)
    south_msg = jnp.concatenate([masked[:, :, half:], fields], axis=1)
    below = halo(north_msg, "geo", 0, SUBSTEPS, -1)
    above = halo(south_msg, "geo", 0, SUBSTEPS, +1)

    group_speed, orbit_weight = physics(radian_freq, water_depth, dir_count)
    partial_value = jnp.sum(orbit_weight * jnp.sum(energy, axis=2), axis=1)

    freq_index = lax.axis_index("freq")
    freq_total = lax.axis_size("freq")
    slot = jnp.zeros((tile_rows, 1, dir_count, tile_cols), jnp.float32)
    slot = slot.at[:, 0, 0, :].set(partial_value)

    def tagged_halo(side):
        pieces = []
        distance = 1
        need = 2 * FH
        while need > 0:
            take = min(freq_count, need)
            lo = freq_count - take if side < 0 else 0
            piece = jnp.concatenate(
                [lax.slice_in_dim(masked, lo, lo + take, axis=1), slot], axis=1
            )
            got = from_neighbour(piece, "freq", -side * distance, True)
            source = freq_index + side * distance
            inside = (source >= 0) & (source < freq_total)
            pieces.append(
                (distance * side, jnp.where(inside, got[:, :take], 0.0), got[:, take, 0, :])
            )
            need -= take
            distance += 1
        return pieces

    low = tagged_halo(-1)
    high = tagged_halo(+1)
    low_bins = [p[1] for p in reversed(low)]
    high_bins = [p[1] for p in high]
    known = {0: partial_value}
    for offset, _, value in low + high:
        known[offset] = value
    orbital = jnp.sqrt(gathered_sum(known, freq_index, freq_total, partial_value))
    full_step = SUBSTEPS * sub_step
    damping = 1.0 + full_step * canopy * veg_field * orbital

    extended = jnp.concatenate(low_bins + [masked] + high_bins, axis=1)
    change = source_change(extended, quad_offsets, quad_weights, freq_count)
    increment = (masked + full_step * change) / damping[:, None, None, :] - masked

    geo_index = lax.axis_index("geo")
    geo_count = lax.axis_size("geo")

    def unpack(parts, offsets):
        spectra, speeds, wets = [], [], []
        for part, offset in zip(parts, offsets):
            valid = (geo_index + offset >= 0) & (geo_index + offset < geo_count)
            depth = jnp.where(valid, part[:, freq_count, 1, :], 1.0)
            spectra.append(part[:, :freq_count])
            wets.append(part[:, freq_count, 0, :])
            speeds.append(physics(radian_freq, depth, dir_count)[0])
        return spectra, speeds, wets

    n_off = [-(len(below) - k) for k in range(len(below))]
    b_spec, b_speed, b_wet = unpack(below, n_off)
    north = propagate(
        jnp.concatenate(b_spec + [masked[:, :, :half]], axis=0),
        jnp.concatenate(b_speed + [group_speed], axis=0),
        jnp.concatenate(b_wet + [wet_field], axis=0),
        cosines[:half],
        sines[:half],
        True,
    )
    s_off = [k + 1 for k in range(len(above))]
    a_spec, a_speed, a_wet = unpack(above, s_off)
    south = propagate(
        jnp.concatenate([masked[:, :, half:]] + a_spec, axis=0),
        jnp.concatenate([group_speed] + a_speed, axis=0),
        jnp.concatenate([wet_field] + a_wet, axis=0),
        cosines[half:],
        sines[half:],
        False,
    )
    moved = jnp.concatenate([north, south], axis=2)
    return (wet_four * (moved + increment), orbital)


def solution(mesh):
    placed = (
        P("geo", "freq", None, None),
        P("geo", None),
        P("geo", None),
        P("geo", None),
        P("geo", None),
        P(),
        P(),
    )
    return jax.shard_map(
        body,
        mesh=mesh,
        in_specs=placed,
        out_specs=(P("geo", "freq", None, None), P("geo", None)),
        check_vma=False,
    )
```

```python
import math

import jax
import jax.numpy as jnp
from jax import lax
from jax.sharding import PartitionSpec as P

FH = 4
SUBSTEPS = 8


gravity = 9.81
base_freq = 0.03
freq_ratio = 1.05
cell_size = 20.0
sub_step = 2.0
coupling = 0.01
coef_plus = 0.4096
coef_minus = 3.1605
coef_both = 2.589


def from_neighbour(block, axis, distance, cyclic=False):
    count = lax.axis_size(axis)
    if cyclic:
        pairs = [(i, (i + distance) % count) for i in range(count)]
    else:
        pairs = [(i, i + distance) for i in range(count) if 0 <= i + distance < count]
    return lax.ppermute(block, axis, pairs)


def halo(block, axis, dim, width, side, cyclic=False):
    size = block.shape[dim]
    parts = []
    distance = 1
    need = width
    while need > 0:
        take = min(size, need)
        if side < 0:
            piece = lax.slice_in_dim(block, size - take, size, axis=dim)
            parts.insert(0, from_neighbour(piece, axis, distance, cyclic))
        else:
            piece = lax.slice_in_dim(block, 0, take, axis=dim)
            parts.append(from_neighbour(piece, axis, -distance, cyclic))
        need -= take
        distance += 1
    return parts


def butterfly_sum(value, axis):
    count = lax.axis_size(axis)
    assert count & (count - 1) == 0
    step = 1
    while step < count:
        value = value + lax.ppermute(value, axis, [(i, i ^ step) for i in range(count)])
        step *= 2
    return value


def gathered_sum(known, index, count, value):
    reach = max(known)
    if count > 2 * (2 * reach + 1) - 2 or count % 2:
        return butterfly_sum(value, "freq")
    far = count // 2
    ordered = jnp.stack([known[o] for o in range(-reach, reach + 1)])
    more = from_neighbour(ordered, "freq", far, True)
    table = []
    for rel in range(count):
        off = rel if rel <= reach else rel - count
        if -reach <= off <= reach:
            table.append(known[off])
        else:
            table.append(more[rel - far + reach])
    table = jnp.stack(table)
    table = jnp.concatenate([table, table], axis=0)
    start = (count - index) % count
    glob = lax.dynamic_slice_in_dim(table, start, count, axis=0)
    while glob.shape[0] > 1:
        glob = glob[0::2] + glob[1::2]
    return glob[0]


def physics(radian_freq, water_depth, dir_count):
    square = (radian_freq * radian_freq)[None, :, None]
    column = water_depth[:, None, :]
    depth_ratio = square * column / gravity
    depth_wave = depth_ratio / jnp.sqrt(jnp.tanh(depth_ratio))
    group_speed = (
        radian_freq[None, :, None]
        * column
        / depth_wave
        * (0.5 + depth_wave / jnp.sinh(2.0 * depth_wave))
    )
    orbit_weight = (
        square
        / jnp.sinh(depth_wave) ** 2
        * (radian_freq * (freq_ratio - 1.0))[None, :, None]
        * (2.0 * math.pi / dir_count)
    )
    return (group_speed, orbit_weight)


def angles_of(dir_count):
    angles = (jnp.arange(dir_count, dtype=jnp.float32) + 0.5) * (2.0 * math.pi / dir_count)
    return (jnp.cos(angles), jnp.sin(angles))


def shifted(doubled, freq_start, dir_off, count):
    dir_count = doubled.shape[2] // 2
    starts = (
        jnp.zeros((), jnp.int32),
        freq_start,
        dir_off % dir_count,
        jnp.zeros((), jnp.int32),
    )
    return lax.dynamic_slice(
        doubled, starts, (doubled.shape[0], count, dir_count, doubled.shape[3])
    )


def source_change(extended, quad_offsets, quad_weights, count):
    up_bins, down_bins, up_turn, down_turn = (
        quad_offsets[0],
        quad_offsets[1],
        quad_offsets[2],
        quad_offsets[3],
    )
    weight_up, weight_down = (quad_weights[0], quad_weights[1])
    wide = count + 2 * FH
    doubled = jnp.concatenate([extended, extended], axis=2)
    centre = lax.slice_in_dim(extended, FH, FH + wide, axis=1)
    upper = weight_up * shifted(doubled, FH + up_bins, up_turn, wide) + (
        1.0 - weight_up
    ) * shifted(doubled, FH + up_bins + 1, up_turn, wide)
    lower = weight_down * shifted(doubled, FH - down_bins, -down_turn, wide) + (
        1.0 - weight_down
    ) * shifted(doubled, FH - down_bins - 1, -down_turn, wide)
    transfer = coupling * (
        centre * centre * (coef_plus * upper + coef_minus * lower)
        - coef_both * centre * upper * lower
    )
    spread = jnp.concatenate([transfer, transfer], axis=2)
    gained = weight_up * shifted(spread, FH - up_bins, -up_turn, count) + (
        1.0 - weight_up
    ) * shifted(spread, FH - up_bins - 1, -up_turn, count)
    gained = (
        gained
        + weight_down * shifted(spread, FH + down_bins, down_turn, count)
        + (1.0 - weight_down) * shifted(spread, FH + down_bins + 1, down_turn, count)
    )
    own = lax.slice_in_dim(transfer, FH, FH + count, axis=1)
    return gained - 2.0 * own


def east_west(east_flux, cosines):
    zeros = jnp.zeros_like(east_flux[..., :1])
    behind = jnp.concatenate([zeros, east_flux[..., :-1]], axis=-1)
    ahead = jnp.concatenate([east_flux[..., 1:], zeros], axis=-1)
    east_going = (cosines > 0.0)[None, None, :, None]
    return jnp.where(east_going, east_flux - behind, ahead - east_flux)


def propagate(spectrum, speed, wet, cosines, sines, northward):
    step_ratio = sub_step / cell_size
    east_speed = speed[:, :, None, :] * cosines[None, None, :, None]
    north_speed = speed[:, :, None, :] * sines[None, None, :, None]
    rows = spectrum.shape[0]
    for substep in range(SUBSTEPS):
        lo, hi = (substep, rows) if northward else (0, rows - substep)
        east_flux = east_speed[lo:hi] * spectrum
        north_flux = north_speed[lo:hi] * spectrum
        along = north_flux[1:] - north_flux[:-1]
        across = east_west(east_flux, cosines)
        if northward:
            spectrum = wet[lo + 1 : hi, None, None, :] * (
                spectrum[1:] - step_ratio * (across[1:] + along)
            )
        else:
            spectrum = wet[lo : hi - 1, None, None, :] * (
                spectrum[:-1] - step_ratio * (across[:-1] + along)
            )
    return spectrum


def body(energy, water_depth, wet_mask, vegetation, canopy, quad_offsets, quad_weights):
    tile_rows, freq_count, dir_count, tile_cols = energy.shape
    wet_field = wet_mask.astype(jnp.float32)
    veg_field = vegetation.astype(jnp.float32)
    wet_four = wet_field[:, None, None, :]
    masked = wet_four * energy
    first_bin = lax.axis_index("freq") * freq_count
    bin_index = (first_bin + jnp.arange(freq_count, dtype=jnp.int32)).astype(jnp.float32)
    radian_freq = 2.0 * math.pi * base_freq * jnp.power(freq_ratio, bin_index)
    half = dir_count // 2
    cosines, sines = angles_of(dir_count)

    fields = jnp.zeros((tile_rows, 1, half, tile_cols), jnp.float32)
    fields = fields.at[:, 0, 0, :].set(wet_field).at[:, 0, 1, :].set(water_depth)
    north_msg = jnp.concatenate([masked[:, :, :half], fields], axis=1)
    south_msg = jnp.concatenate([masked[:, :, half:], fields], axis=1)
    below = halo(north_msg, "geo", 0, SUBSTEPS, -1)
    above = halo(south_msg, "geo", 0, SUBSTEPS, +1)

    group_speed, orbit_weight = physics(radian_freq, water_depth, dir_count)
    partial_value = jnp.sum(orbit_weight * jnp.sum(energy, axis=2), axis=1)

    freq_index = lax.axis_index("freq")
    freq_total = lax.axis_size("freq")
    slot = jnp.zeros((tile_rows, 1, dir_count, tile_cols), jnp.float32)
    slot = slot.at[:, 0, 0, :].set(partial_value)
    gathered = lax.all_gather(jnp.concatenate([masked, slot], axis=1), "freq", axis=1, tiled=True)
    gathered = gathered.reshape(tile_rows, freq_total, freq_count + 1, dir_count, tile_cols)
    partials = gathered[:, :, freq_count, 0, :]
    spectrum_all = gathered[:, :, :freq_count].reshape(
        tile_rows, freq_total * freq_count, dir_count, tile_cols
    )
    padded_all = jnp.pad(spectrum_all, ((0, 0), (2 * FH, 2 * FH), (0, 0), (0, 0)))
    extended = lax.dynamic_slice_in_dim(padded_all, first_bin, freq_count + 4 * FH, axis=1)
    glob = jnp.moveaxis(partials, 1, 0)
    while glob.shape[0] > 1:
        glob = glob[0::2] + glob[1::2]
    orbital = jnp.sqrt(glob[0])
    full_step = SUBSTEPS * sub_step
    damping = 1.0 + full_step * canopy * veg_field * orbital

    change = source_change(extended, quad_offsets, quad_weights, freq_count)
    increment = (masked + full_step * change) / damping[:, None, None, :] - masked

    geo_index = lax.axis_index("geo")
    geo_count = lax.axis_size("geo")

    def unpack(parts, offsets):
        spectra, speeds, wets = [], [], []
        for part, offset in zip(parts, offsets):
            valid = (geo_index + offset >= 0) & (geo_index + offset < geo_count)
            depth = jnp.where(valid, part[:, freq_count, 1, :], 1.0)
            spectra.append(part[:, :freq_count])
            wets.append(part[:, freq_count, 0, :])
            speeds.append(physics(radian_freq, depth, dir_count)[0])
        return spectra, speeds, wets

    n_off = [-(len(below) - k) for k in range(len(below))]
    b_spec, b_speed, b_wet = unpack(below, n_off)
    north = propagate(
        jnp.concatenate(b_spec + [masked[:, :, :half]], axis=0),
        jnp.concatenate(b_speed + [group_speed], axis=0),
        jnp.concatenate(b_wet + [wet_field], axis=0),
        cosines[:half],
        sines[:half],
        True,
    )
    s_off = [k + 1 for k in range(len(above))]
    a_spec, a_speed, a_wet = unpack(above, s_off)
    south = propagate(
        jnp.concatenate([masked[:, :, half:]] + a_spec, axis=0),
        jnp.concatenate([group_speed] + a_speed, axis=0),
        jnp.concatenate([wet_field] + a_wet, axis=0),
        cosines[half:],
        sines[half:],
        False,
    )
    moved = jnp.concatenate([north, south], axis=2)
    return (wet_four * (moved + increment), orbital)


def solution(mesh):
    placed = (
        P("geo", "freq", None, None),
        P("geo", None),
        P("geo", None),
        P("geo", None),
        P("geo", None),
        P(),
        P(),
    )
    return jax.shard_map(
        body,
        mesh=mesh,
        in_specs=placed,
        out_specs=(P("geo", "freq", None, None), P("geo", None)),
        check_vma=False,
    )
```

```python
import math

import jax
import jax.numpy as jnp
from jax import lax
from jax.sharding import PartitionSpec as P

FH = 4
SUBSTEPS = 8


gravity = 9.81
base_freq = 0.03
freq_ratio = 1.05
cell_size = 20.0
sub_step = 2.0
coupling = 0.01
coef_plus = 0.4096
coef_minus = 3.1605
coef_both = 2.589


def from_neighbour(block, axis, distance, cyclic=False):
    count = lax.axis_size(axis)
    if cyclic:
        pairs = [(i, (i + distance) % count) for i in range(count)]
    else:
        pairs = [(i, i + distance) for i in range(count) if 0 <= i + distance < count]
    return lax.ppermute(block, axis, pairs)


def halo(block, axis, dim, width, side, cyclic=False):
    size = block.shape[dim]
    parts = []
    distance = 1
    need = width
    while need > 0:
        take = min(size, need)
        if side < 0:
            piece = lax.slice_in_dim(block, size - take, size, axis=dim)
            parts.insert(0, from_neighbour(piece, axis, distance, cyclic))
        else:
            piece = lax.slice_in_dim(block, 0, take, axis=dim)
            parts.append(from_neighbour(piece, axis, -distance, cyclic))
        need -= take
        distance += 1
    return parts


def butterfly_sum(value, axis):
    count = lax.axis_size(axis)
    assert count & (count - 1) == 0
    step = 1
    while step < count:
        value = value + lax.ppermute(value, axis, [(i, i ^ step) for i in range(count)])
        step *= 2
    return value


def gathered_sum(known, index, count, value):
    reach = max(known)
    if count > 2 * (2 * reach + 1) - 2 or count % 2:
        return butterfly_sum(value, "freq")
    far = count // 2
    ordered = jnp.stack([known[o] for o in range(-reach, reach + 1)])
    more = from_neighbour(ordered, "freq", far, True)
    table = []
    for rel in range(count):
        off = rel if rel <= reach else rel - count
        if -reach <= off <= reach:
            table.append(known[off])
        else:
            table.append(more[rel - far + reach])
    table = jnp.stack(table)
    table = jnp.concatenate([table, table], axis=0)
    start = (count - index) % count
    glob = lax.dynamic_slice_in_dim(table, start, count, axis=0)
    while glob.shape[0] > 1:
        glob = glob[0::2] + glob[1::2]
    return glob[0]


def physics(radian_freq, water_depth, dir_count):
    square = (radian_freq * radian_freq)[None, :, None]
    column = water_depth[:, None, :]
    depth_ratio = square * column / gravity
    depth_wave = depth_ratio / jnp.sqrt(jnp.tanh(depth_ratio))
    group_speed = (
        radian_freq[None, :, None]
        * column
        / depth_wave
        * (0.5 + depth_wave / jnp.sinh(2.0 * depth_wave))
    )
    orbit_weight = (
        square
        / jnp.sinh(depth_wave) ** 2
        * (radian_freq * (freq_ratio - 1.0))[None, :, None]
        * (2.0 * math.pi / dir_count)
    )
    return (group_speed, orbit_weight)


def angles_of(dir_count):
    angles = (jnp.arange(dir_count, dtype=jnp.float32) + 0.5) * (2.0 * math.pi / dir_count)
    return (jnp.cos(angles), jnp.sin(angles))


def shifted(doubled, freq_start, dir_off, count):
    dir_count = doubled.shape[2] // 2
    starts = (
        jnp.zeros((), jnp.int32),
        freq_start,
        dir_off % dir_count,
        jnp.zeros((), jnp.int32),
    )
    return lax.dynamic_slice(
        doubled, starts, (doubled.shape[0], count, dir_count, doubled.shape[3])
    )


def interaction(extended, masked, quad_offsets, quad_weights):
    count = masked.shape[1]
    doubled = jnp.concatenate([extended, extended], axis=2)
    up_bins, down_bins, up_turn, down_turn = (
        quad_offsets[0],
        quad_offsets[1],
        quad_offsets[2],
        quad_offsets[3],
    )
    weight_up, weight_down = (quad_weights[0], quad_weights[1])
    upper = weight_up * shifted(doubled, FH + up_bins, up_turn, count) + (
        1.0 - weight_up
    ) * shifted(doubled, FH + up_bins + 1, up_turn, count)
    lower = weight_down * shifted(doubled, FH - down_bins, -down_turn, count) + (
        1.0 - weight_down
    ) * shifted(doubled, FH - down_bins - 1, -down_turn, count)
    return coupling * (
        masked * masked * (coef_plus * upper + coef_minus * lower)
        - coef_both * masked * upper * lower
    )


def redistribute(extended, transfer, quad_offsets, quad_weights):
    count = transfer.shape[1]
    doubled = jnp.concatenate([extended, extended], axis=2)
    up_bins, down_bins, up_turn, down_turn = (
        quad_offsets[0],
        quad_offsets[1],
        quad_offsets[2],
        quad_offsets[3],
    )
    weight_up, weight_down = (quad_weights[0], quad_weights[1])
    gained = weight_up * shifted(doubled, FH - up_bins, -up_turn, count) + (
        1.0 - weight_up
    ) * shifted(doubled, FH - up_bins - 1, -up_turn, count)
    gained = (
        gained
        + weight_down * shifted(doubled, FH + down_bins, down_turn, count)
        + (1.0 - weight_down) * shifted(doubled, FH + down_bins + 1, down_turn, count)
    )
    return gained - 2.0 * transfer


def east_west(east_flux, cosines):
    zeros = jnp.zeros_like(east_flux[..., :1])
    behind = jnp.concatenate([zeros, east_flux[..., :-1]], axis=-1)
    ahead = jnp.concatenate([east_flux[..., 1:], zeros], axis=-1)
    east_going = (cosines > 0.0)[None, None, :, None]
    return jnp.where(east_going, east_flux - behind, ahead - east_flux)


def propagate(spectrum, speed, wet, cosines, sines, northward, substeps):
    step_ratio = sub_step / cell_size
    east_speed = speed[:, :, None, :] * cosines[None, None, :, None]
    north_speed = speed[:, :, None, :] * sines[None, None, :, None]
    rows = spectrum.shape[0]
    for substep in range(substeps):
        lo, hi = (substep, rows) if northward else (0, rows - substep)
        east_flux = east_speed[lo:hi] * spectrum
        north_flux = north_speed[lo:hi] * spectrum
        along = north_flux[1:] - north_flux[:-1]
        across = east_west(east_flux, cosines)
        if northward:
            spectrum = wet[lo + 1 : hi, None, None, :] * (
                spectrum[1:] - step_ratio * (across[1:] + along)
            )
        else:
            spectrum = wet[lo : hi - 1, None, None, :] * (
                spectrum[:-1] - step_ratio * (across[:-1] + along)
            )
    return spectrum


def tagged_exchange(block, tags, axis, width):
    rows, bins, dirs, cols = block.shape
    index = lax.axis_index(axis)
    count = lax.axis_size(axis)
    slot = jnp.zeros((rows, 1, dirs, cols), jnp.float32)
    for k in range(tags.shape[0]):
        slot = slot.at[:, 0, k, :].set(tags[k])
    got = {}
    for side in (-1, 1):
        lo = bins - width if side < 0 else 0
        piece = jnp.concatenate([lax.slice_in_dim(block, lo, lo + width, axis=1), slot], axis=1)
        recv = from_neighbour(piece, axis, -side, True)
        source = index + side
        inside = (source >= 0) & (source < count)
        got[side] = (
            jnp.where(inside, recv[:, :width], 0.0),
            [recv[:, width, k, :] for k in range(tags.shape[0])],
        )
    return got


def body(energy, water_depth, wet_mask, vegetation, canopy, quad_offsets, quad_weights):
    tile_rows, freq_count, dir_count, tile_cols = energy.shape
    wet_field = wet_mask.astype(jnp.float32)
    veg_field = vegetation.astype(jnp.float32)
    wet_four = wet_field[:, None, None, :]
    masked = wet_four * energy
    freq_index = lax.axis_index("freq")
    freq_total = lax.axis_size("freq")
    first_bin = freq_index * freq_count
    bin_index = (first_bin + jnp.arange(freq_count, dtype=jnp.int32)).astype(jnp.float32)
    radian_freq = 2.0 * math.pi * base_freq * jnp.power(freq_ratio, bin_index)
    half = dir_count // 2
    cosines, sines = angles_of(dir_count)
    group_speed, orbit_weight = physics(radian_freq, water_depth, dir_count)
    partial_value = jnp.sum(orbit_weight * jnp.sum(energy, axis=2), axis=1)
    geo_index = lax.axis_index("geo")
    geo_count = lax.axis_size("geo")
    first_half = SUBSTEPS // 2
    assert tile_rows >= first_half and SUBSTEPS - first_half <= tile_rows

    fields = jnp.zeros((tile_rows, 1, half, tile_cols), jnp.float32)
    fields = fields.at[:, 0, 0, :].set(wet_field).at[:, 0, 1, :].set(water_depth)
    north_msg = jnp.concatenate([masked[:, :, :half], fields], axis=1)
    south_msg = jnp.concatenate([masked[:, :, half:], fields], axis=1)
    below = from_neighbour(north_msg, "geo", 1)
    above = from_neighbour(south_msg, "geo", -1)
    spectrum_halo = tagged_exchange(masked, partial_value[None], "freq", FH)

    def rim(part, offset):
        valid = (geo_index + offset >= 0) & (geo_index + offset < geo_count)
        depth = jnp.where(valid, part[:, freq_count, 1, :], 1.0)
        return part[:, :freq_count], physics(radian_freq, depth, dir_count)[0], part[:, freq_count, 0, :]

    b_spec, b_speed, b_wet = rim(below, -1)
    a_spec, a_speed, a_wet = rim(above, 1)
    north_speed = jnp.concatenate([b_speed, group_speed], axis=0)
    north_wet = jnp.concatenate([b_wet, wet_field], axis=0)
    south_speed = jnp.concatenate([group_speed, a_speed], axis=0)
    south_wet = jnp.concatenate([wet_field, a_wet], axis=0)
    north = propagate(
        jnp.concatenate([b_spec[tile_rows - first_half :], masked[:, :, :half]], axis=0),
        north_speed[tile_rows - first_half :],
        north_wet[tile_rows - first_half :],
        cosines[:half],
        sines[:half],
        True,
        first_half,
    )
    south = propagate(
        jnp.concatenate([masked[:, :, half:], a_spec[:first_half]], axis=0),
        south_speed[: 2 * tile_rows - (tile_rows - first_half)],
        south_wet[: 2 * tile_rows - (tile_rows - first_half)],
        cosines[half:],
        sines[half:],
        False,
        first_half,
    )
    extended = jnp.concatenate([spectrum_halo[-1][0], masked, spectrum_halo[1][0]], axis=1)
    transfer = interaction(extended, masked, quad_offsets, quad_weights)
    known = {0: partial_value, -1: spectrum_halo[-1][1][0], 1: spectrum_halo[1][1][0]}

    second = SUBSTEPS - first_half
    north_mid = from_neighbour(north, "geo", 1)
    south_mid = from_neighbour(south, "geo", -1)
    transfer_halo = tagged_exchange(
        transfer, jnp.stack([known[-1], known[0], known[1]]), "freq", FH
    )
    known[-2] = transfer_halo[-1][1][0]
    known[2] = transfer_halo[1][1][2]
    north = propagate(
        jnp.concatenate([north_mid[tile_rows - second :], north], axis=0),
        north_speed[tile_rows - second :],
        north_wet[tile_rows - second :],
        cosines[:half],
        sines[:half],
        True,
        second,
    )
    south = propagate(
        jnp.concatenate([south, south_mid[:second]], axis=0),
        south_speed[: tile_rows + second],
        south_wet[: tile_rows + second],
        cosines[half:],
        sines[half:],
        False,
        second,
    )
    spread = jnp.concatenate([transfer_halo[-1][0], transfer, transfer_halo[1][0]], axis=1)
    change = redistribute(spread, transfer, quad_offsets, quad_weights)

    orbital = jnp.sqrt(gathered_sum(known, freq_index, freq_total, partial_value))
    full_step = SUBSTEPS * sub_step
    damping = 1.0 + full_step * canopy * veg_field * orbital
    increment = (masked + full_step * change) / damping[:, None, None, :] - masked
    moved = jnp.concatenate([north, south], axis=2)
    return (wet_four * (moved + increment), orbital)


def solution(mesh):
    placed = (
        P("geo", "freq", None, None),
        P("geo", None),
        P("geo", None),
        P("geo", None),
        P("geo", None),
        P(),
        P(),
    )
    return jax.shard_map(
        body,
        mesh=mesh,
        in_specs=placed,
        out_specs=(P("geo", "freq", None, None), P("geo", None)),
        check_vma=False,
    )
```

```python
import math

import jax
import jax.numpy as jnp
from jax import lax
from jax.sharding import PartitionSpec as P

FH = 4
SUBSTEPS = 8


gravity = 9.81
base_freq = 0.03
freq_ratio = 1.05
cell_size = 20.0
sub_step = 2.0
coupling = 0.01
coef_plus = 0.4096
coef_minus = 3.1605
coef_both = 2.589


def from_neighbour(block, axis, distance, cyclic=False):
    count = lax.axis_size(axis)
    if cyclic:
        pairs = [(i, (i + distance) % count) for i in range(count)]
    else:
        pairs = [(i, i + distance) for i in range(count) if 0 <= i + distance < count]
    return lax.ppermute(block, axis, pairs)


def halo(block, axis, dim, width, side, cyclic=False):
    size = block.shape[dim]
    parts = []
    distance = 1
    need = width
    while need > 0:
        take = min(size, need)
        if side < 0:
            piece = lax.slice_in_dim(block, size - take, size, axis=dim)
            parts.insert(0, from_neighbour(piece, axis, distance, cyclic))
        else:
            piece = lax.slice_in_dim(block, 0, take, axis=dim)
            parts.append(from_neighbour(piece, axis, -distance, cyclic))
        need -= take
        distance += 1
    return parts


def butterfly_sum(value, axis):
    count = lax.axis_size(axis)
    assert count & (count - 1) == 0
    step = 1
    while step < count:
        value = value + lax.ppermute(value, axis, [(i, i ^ step) for i in range(count)])
        step *= 2
    return value


def gathered_sum(known, index, count, value):
    reach = max(known)
    if count > 2 * (2 * reach + 1) - 2 or count % 2:
        return butterfly_sum(value, "freq")
    far = count // 2
    ordered = jnp.stack([known[o] for o in range(-reach, reach + 1)])
    more = from_neighbour(ordered, "freq", far, True)
    table = []
    for rel in range(count):
        off = rel if rel <= reach else rel - count
        if -reach <= off <= reach:
            table.append(known[off])
        else:
            table.append(more[rel - far + reach])
    table = jnp.stack(table)
    table = jnp.concatenate([table, table], axis=0)
    start = (count - index) % count
    glob = lax.dynamic_slice_in_dim(table, start, count, axis=0)
    while glob.shape[0] > 1:
        glob = glob[0::2] + glob[1::2]
    return glob[0]


def physics(radian_freq, water_depth, dir_count):
    square = (radian_freq * radian_freq)[None, :, None]
    column = water_depth[:, None, :]
    depth_ratio = square * column / gravity
    depth_wave = depth_ratio / jnp.sqrt(jnp.tanh(depth_ratio))
    group_speed = (
        radian_freq[None, :, None]
        * column
        / depth_wave
        * (0.5 + depth_wave / jnp.sinh(2.0 * depth_wave))
    )
    orbit_weight = (
        square
        / jnp.sinh(depth_wave) ** 2
        * (radian_freq * (freq_ratio - 1.0))[None, :, None]
        * (2.0 * math.pi / dir_count)
    )
    return (group_speed, orbit_weight)


def angles_of(dir_count):
    angles = (jnp.arange(dir_count, dtype=jnp.float32) + 0.5) * (2.0 * math.pi / dir_count)
    return (jnp.cos(angles), jnp.sin(angles))


def shifted(doubled, freq_start, dir_off, count):
    dir_count = doubled.shape[2] // 2
    starts = (
        jnp.zeros((), jnp.int32),
        freq_start,
        dir_off % dir_count,
        jnp.zeros((), jnp.int32),
    )
    return lax.dynamic_slice(
        doubled, starts, (doubled.shape[0], count, dir_count, doubled.shape[3])
    )


def source_change(extended, quad_offsets, quad_weights, count):
    up_bins, down_bins, up_turn, down_turn = (
        quad_offsets[0],
        quad_offsets[1],
        quad_offsets[2],
        quad_offsets[3],
    )
    weight_up, weight_down = (quad_weights[0], quad_weights[1])
    wide = count + 2 * FH
    doubled = jnp.concatenate([extended, extended], axis=2)
    centre = lax.slice_in_dim(extended, FH, FH + wide, axis=1)
    upper = weight_up * shifted(doubled, FH + up_bins, up_turn, wide) + (
        1.0 - weight_up
    ) * shifted(doubled, FH + up_bins + 1, up_turn, wide)
    lower = weight_down * shifted(doubled, FH - down_bins, -down_turn, wide) + (
        1.0 - weight_down
    ) * shifted(doubled, FH - down_bins - 1, -down_turn, wide)
    transfer = coupling * (
        centre * centre * (coef_plus * upper + coef_minus * lower)
        - coef_both * centre * upper * lower
    )
    spread = jnp.concatenate([transfer, transfer], axis=2)
    gained = weight_up * shifted(spread, FH - up_bins, -up_turn, count) + (
        1.0 - weight_up
    ) * shifted(spread, FH - up_bins - 1, -up_turn, count)
    gained = (
        gained
        + weight_down * shifted(spread, FH + down_bins, down_turn, count)
        + (1.0 - weight_down) * shifted(spread, FH + down_bins + 1, down_turn, count)
    )
    own = lax.slice_in_dim(transfer, FH, FH + count, axis=1)
    return gained - 2.0 * own


def east_west(east_flux, cosines):
    zeros = jnp.zeros_like(east_flux[..., :1])
    behind = jnp.concatenate([zeros, east_flux[..., :-1]], axis=-1)
    ahead = jnp.concatenate([east_flux[..., 1:], zeros], axis=-1)
    east_going = (cosines > 0.0)[None, None, :, None]
    return jnp.where(east_going, east_flux - behind, ahead - east_flux)


def propagate(spectrum, speed, wet, cosines, sines, northward):
    step_ratio = sub_step / cell_size
    east_speed = speed[:, :, None, :] * cosines[None, None, :, None]
    north_speed = speed[:, :, None, :] * sines[None, None, :, None]
    rows = spectrum.shape[0]
    for substep in range(SUBSTEPS):
        lo, hi = (substep, rows) if northward else (0, rows - substep)
        east_flux = east_speed[lo:hi] * spectrum
        north_flux = north_speed[lo:hi] * spectrum
        along = north_flux[1:] - north_flux[:-1]
        across = east_west(east_flux, cosines)
        if northward:
            spectrum = wet[lo + 1 : hi, None, None, :] * (
                spectrum[1:] - step_ratio * (across[1:] + along)
            )
        else:
            spectrum = wet[lo : hi - 1, None, None, :] * (
                spectrum[:-1] - step_ratio * (across[:-1] + along)
            )
    return spectrum


def body(energy, water_depth, wet_mask, vegetation, canopy, quad_offsets, quad_weights):
    tile_rows, freq_count, dir_count, tile_cols = energy.shape
    wet_field = wet_mask.astype(jnp.float32)
    veg_field = vegetation.astype(jnp.float32)
    wet_four = wet_field[:, None, None, :]
    masked = wet_four * energy
    first_bin = lax.axis_index("freq") * freq_count
    bin_index = (first_bin + jnp.arange(freq_count, dtype=jnp.int32)).astype(jnp.float32)
    radian_freq = 2.0 * math.pi * base_freq * jnp.power(freq_ratio, bin_index)
    half = dir_count // 2
    cosines, sines = angles_of(dir_count)

    fields = jnp.zeros((tile_rows, 1, half, tile_cols), jnp.float32)
    fields = fields.at[:, 0, 0, :].set(wet_field).at[:, 0, 1, :].set(water_depth)
    north_msg = jnp.concatenate([masked[:, :, :half], fields], axis=1)
    south_msg = jnp.concatenate([masked[:, :, half:], fields], axis=1)

    group_speed, orbit_weight = physics(radian_freq, water_depth, dir_count)
    partial_value = jnp.sum(orbit_weight * jnp.sum(energy, axis=2), axis=1)

    freq_index = lax.axis_index("freq")
    freq_total = lax.axis_size("freq")
    slot = jnp.zeros((tile_rows, 1, dir_count, tile_cols), jnp.float32)
    slot = slot.at[:, 0, 0, :].set(partial_value)

    def tagged_halo(side):
        pieces = []
        distance = 1
        need = 2 * FH
        while need > 0:
            take = min(freq_count, need)
            lo = freq_count - take if side < 0 else 0
            piece = jnp.concatenate(
                [lax.slice_in_dim(masked, lo, lo + take, axis=1), slot], axis=1
            )
            got = from_neighbour(piece, "freq", -side * distance, True)
            source = freq_index + side * distance
            inside = (source >= 0) & (source < freq_total)
            pieces.append(
                (distance * side, jnp.where(inside, got[:, :take], 0.0), got[:, take, 0, :])
            )
            need -= take
            distance += 1
        return pieces

    low = tagged_halo(-1)
    high = tagged_halo(+1)
    arrays = [(p[1], p[2]) for p in low + high]
    north_msg, south_msg, arrays = lax.optimization_barrier((north_msg, south_msg, arrays))
    tagged = [(p[0],) + tuple(a) for p, a in zip(low + high, arrays)]
    low, high = tagged[: len(low)], tagged[len(low) :]
    below = halo(north_msg, "geo", 0, SUBSTEPS, -1)
    above = halo(south_msg, "geo", 0, SUBSTEPS, +1)
    low_bins = [p[1] for p in reversed(low)]
    high_bins = [p[1] for p in high]
    known = {0: partial_value}
    for offset, _, value in low + high:
        known[offset] = value
    orbital = jnp.sqrt(gathered_sum(known, freq_index, freq_total, partial_value))
    full_step = SUBSTEPS * sub_step
    damping = 1.0 + full_step * canopy * veg_field * orbital

    extended = jnp.concatenate(low_bins + [masked] + high_bins, axis=1)
    change = source_change(extended, quad_offsets, quad_weights, freq_count)
    increment = (masked + full_step * change) / damping[:, None, None, :] - masked

    geo_index = lax.axis_index("geo")
    geo_count = lax.axis_size("geo")

    def unpack(parts, offsets):
        spectra, speeds, wets = [], [], []
        for part, offset in zip(parts, offsets):
            valid = (geo_index + offset >= 0) & (geo_index + offset < geo_count)
            depth = jnp.where(valid, part[:, freq_count, 1, :], 1.0)
            spectra.append(part[:, :freq_count])
            wets.append(part[:, freq_count, 0, :])
            speeds.append(physics(radian_freq, depth, dir_count)[0])
        return spectra, speeds, wets

    n_off = [-(len(below) - k) for k in range(len(below))]
    b_spec, b_speed, b_wet = unpack(below, n_off)
    north = propagate(
        jnp.concatenate(b_spec + [masked[:, :, :half]], axis=0),
        jnp.concatenate(b_speed + [group_speed], axis=0),
        jnp.concatenate(b_wet + [wet_field], axis=0),
        cosines[:half],
        sines[:half],
        True,
    )
    s_off = [k + 1 for k in range(len(above))]
    a_spec, a_speed, a_wet = unpack(above, s_off)
    south = propagate(
        jnp.concatenate([masked[:, :, half:]] + a_spec, axis=0),
        jnp.concatenate([group_speed] + a_speed, axis=0),
        jnp.concatenate([wet_field] + a_wet, axis=0),
        cosines[half:],
        sines[half:],
        False,
    )
    moved = jnp.concatenate([north, south], axis=2)
    return (wet_four * (moved + increment), orbital)


def solution(mesh):
    placed = (
        P("geo", "freq", None, None),
        P("geo", None),
        P("geo", None),
        P("geo", None),
        P("geo", None),
        P(),
        P(),
    )
    return jax.shard_map(
        body,
        mesh=mesh,
        in_specs=placed,
        out_specs=(P("geo", "freq", None, None), P("geo", None)),
        check_vma=False,
    )
```

```python
import math

import jax
import jax.numpy as jnp
from jax import lax
from jax.sharding import PartitionSpec as P

FH = 4
SUBSTEPS = 8


gravity = 9.81
base_freq = 0.03
freq_ratio = 1.05
cell_size = 20.0
sub_step = 2.0
coupling = 0.01
coef_plus = 0.4096
coef_minus = 3.1605
coef_both = 2.589


def from_neighbour(block, axis, distance, cyclic=False):
    count = lax.axis_size(axis)
    if cyclic:
        pairs = [(i, (i + distance) % count) for i in range(count)]
    else:
        pairs = [(i, i + distance) for i in range(count) if 0 <= i + distance < count]
    return lax.ppermute(block, axis, pairs)


def halo(block, axis, dim, width, side, cyclic=False):
    size = block.shape[dim]
    parts = []
    distance = 1
    need = width
    while need > 0:
        take = min(size, need)
        if side < 0:
            piece = lax.slice_in_dim(block, size - take, size, axis=dim)
            parts.insert(0, from_neighbour(piece, axis, distance, cyclic))
        else:
            piece = lax.slice_in_dim(block, 0, take, axis=dim)
            parts.append(from_neighbour(piece, axis, -distance, cyclic))
        need -= take
        distance += 1
    return parts


def butterfly_sum(value, axis):
    count = lax.axis_size(axis)
    assert count & (count - 1) == 0
    step = 1
    while step < count:
        value = value + lax.ppermute(value, axis, [(i, i ^ step) for i in range(count)])
        step *= 2
    return value


def gathered_sum(known, index, count, value):
    reach = max(known)
    if count > 2 * (2 * reach + 1) - 2 or count % 2:
        return butterfly_sum(value, "freq")
    far = count // 2
    ordered = jnp.stack([known[o] for o in range(-reach, reach + 1)])
    more = from_neighbour(ordered, "freq", far, True)
    table = []
    for rel in range(count):
        off = rel if rel <= reach else rel - count
        if -reach <= off <= reach:
            table.append(known[off])
        else:
            table.append(more[rel - far + reach])
    table = jnp.stack(table)
    table = jnp.concatenate([table, table], axis=0)
    start = (count - index) % count
    glob = lax.dynamic_slice_in_dim(table, start, count, axis=0)
    while glob.shape[0] > 1:
        glob = glob[0::2] + glob[1::2]
    return glob[0]


def physics(radian_freq, water_depth, dir_count):
    square = (radian_freq * radian_freq)[None, :, None]
    column = water_depth[:, None, :]
    depth_ratio = square * column / gravity
    depth_wave = depth_ratio / jnp.sqrt(jnp.tanh(depth_ratio))
    group_speed = (
        radian_freq[None, :, None]
        * column
        / depth_wave
        * (0.5 + depth_wave / jnp.sinh(2.0 * depth_wave))
    )
    orbit_weight = (
        square
        / jnp.sinh(depth_wave) ** 2
        * (radian_freq * (freq_ratio - 1.0))[None, :, None]
        * (2.0 * math.pi / dir_count)
    )
    return (group_speed, orbit_weight)


def angles_of(dir_count):
    angles = (jnp.arange(dir_count, dtype=jnp.float32) + 0.5) * (2.0 * math.pi / dir_count)
    return (jnp.cos(angles), jnp.sin(angles))


def shifted(doubled, freq_start, dir_off, count):
    dir_count = doubled.shape[2] // 2
    starts = (
        jnp.zeros((), jnp.int32),
        freq_start,
        dir_off % dir_count,
        jnp.zeros((), jnp.int32),
    )
    return lax.dynamic_slice(
        doubled, starts, (doubled.shape[0], count, dir_count, doubled.shape[3])
    )


def interaction(extended, masked, quad_offsets, quad_weights):
    count = masked.shape[1]
    doubled = jnp.concatenate([extended, extended], axis=2)
    up_bins, down_bins, up_turn, down_turn = (
        quad_offsets[0],
        quad_offsets[1],
        quad_offsets[2],
        quad_offsets[3],
    )
    weight_up, weight_down = (quad_weights[0], quad_weights[1])
    upper = weight_up * shifted(doubled, FH + up_bins, up_turn, count) + (
        1.0 - weight_up
    ) * shifted(doubled, FH + up_bins + 1, up_turn, count)
    lower = weight_down * shifted(doubled, FH - down_bins, -down_turn, count) + (
        1.0 - weight_down
    ) * shifted(doubled, FH - down_bins - 1, -down_turn, count)
    return coupling * (
        masked * masked * (coef_plus * upper + coef_minus * lower)
        - coef_both * masked * upper * lower
    )


def redistribute(extended, transfer, quad_offsets, quad_weights):
    count = transfer.shape[1]
    doubled = jnp.concatenate([extended, extended], axis=2)
    up_bins, down_bins, up_turn, down_turn = (
        quad_offsets[0],
        quad_offsets[1],
        quad_offsets[2],
        quad_offsets[3],
    )
    weight_up, weight_down = (quad_weights[0], quad_weights[1])
    gained = weight_up * shifted(doubled, FH - up_bins, -up_turn, count) + (
        1.0 - weight_up
    ) * shifted(doubled, FH - up_bins - 1, -up_turn, count)
    gained = (
        gained
        + weight_down * shifted(doubled, FH + down_bins, down_turn, count)
        + (1.0 - weight_down) * shifted(doubled, FH + down_bins + 1, down_turn, count)
    )
    return gained - 2.0 * transfer


def east_west(east_flux, cosines):
    zeros = jnp.zeros_like(east_flux[..., :1])
    behind = jnp.concatenate([zeros, east_flux[..., :-1]], axis=-1)
    ahead = jnp.concatenate([east_flux[..., 1:], zeros], axis=-1)
    east_going = (cosines > 0.0)[None, None, :, None]
    return jnp.where(east_going, east_flux - behind, ahead - east_flux)


def propagate(spectrum, speed, wet, cosines, sines, northward, substeps):
    step_ratio = sub_step / cell_size
    east_speed = speed[:, :, None, :] * cosines[None, None, :, None]
    north_speed = speed[:, :, None, :] * sines[None, None, :, None]
    rows = spectrum.shape[0]
    for substep in range(substeps):
        lo, hi = (substep, rows) if northward else (0, rows - substep)
        east_flux = east_speed[lo:hi] * spectrum
        north_flux = north_speed[lo:hi] * spectrum
        along = north_flux[1:] - north_flux[:-1]
        across = east_west(east_flux, cosines)
        if northward:
            spectrum = wet[lo + 1 : hi, None, None, :] * (
                spectrum[1:] - step_ratio * (across[1:] + along)
            )
        else:
            spectrum = wet[lo : hi - 1, None, None, :] * (
                spectrum[:-1] - step_ratio * (across[:-1] + along)
            )
    return spectrum


def tagged_exchange(block, tags, axis, width):
    rows, bins, dirs, cols = block.shape
    index = lax.axis_index(axis)
    count = lax.axis_size(axis)
    slot = jnp.zeros((rows, 1, dirs, cols), jnp.float32)
    for k in range(tags.shape[0]):
        slot = slot.at[:, 0, k, :].set(tags[k])
    got = {}
    for side in (-1, 1):
        lo = bins - width if side < 0 else 0
        piece = jnp.concatenate([lax.slice_in_dim(block, lo, lo + width, axis=1), slot], axis=1)
        recv = from_neighbour(piece, axis, -side, True)
        source = index + side
        inside = (source >= 0) & (source < count)
        got[side] = (
            jnp.where(inside, recv[:, :width], 0.0),
            [recv[:, width, k, :] for k in range(tags.shape[0])],
        )
    return got


def body(energy, water_depth, wet_mask, vegetation, canopy, quad_offsets, quad_weights):
    tile_rows, freq_count, dir_count, tile_cols = energy.shape
    wet_field = wet_mask.astype(jnp.float32)
    veg_field = vegetation.astype(jnp.float32)
    wet_four = wet_field[:, None, None, :]
    masked = wet_four * energy
    freq_index = lax.axis_index("freq")
    freq_total = lax.axis_size("freq")
    first_bin = freq_index * freq_count
    bin_index = (first_bin + jnp.arange(freq_count, dtype=jnp.int32)).astype(jnp.float32)
    radian_freq = 2.0 * math.pi * base_freq * jnp.power(freq_ratio, bin_index)
    half = dir_count // 2
    cosines, sines = angles_of(dir_count)
    group_speed, orbit_weight = physics(radian_freq, water_depth, dir_count)
    partial_value = jnp.sum(orbit_weight * jnp.sum(energy, axis=2), axis=1)
    geo_index = lax.axis_index("geo")
    geo_count = lax.axis_size("geo")
    first_half = SUBSTEPS // 2
    assert tile_rows >= first_half and SUBSTEPS - first_half <= tile_rows

    fields = jnp.zeros((tile_rows, 1, half, tile_cols), jnp.float32)
    fields = fields.at[:, 0, 0, :].set(wet_field).at[:, 0, 1, :].set(water_depth)
    north_msg = jnp.concatenate([masked[:, :, :half], fields], axis=1)
    south_msg = jnp.concatenate([masked[:, :, half:], fields], axis=1)
    below = from_neighbour(north_msg, "geo", 1)
    above = from_neighbour(south_msg, "geo", -1)
    spectrum_halo = tagged_exchange(masked, partial_value[None], "freq", FH)
    below, above, spectrum_halo = lax.optimization_barrier((below, above, spectrum_halo))

    def rim(part, offset):
        valid = (geo_index + offset >= 0) & (geo_index + offset < geo_count)
        depth = jnp.where(valid, part[:, freq_count, 1, :], 1.0)
        return part[:, :freq_count], physics(radian_freq, depth, dir_count)[0], part[:, freq_count, 0, :]

    b_spec, b_speed, b_wet = rim(below, -1)
    a_spec, a_speed, a_wet = rim(above, 1)
    north_speed = jnp.concatenate([b_speed, group_speed], axis=0)
    north_wet = jnp.concatenate([b_wet, wet_field], axis=0)
    south_speed = jnp.concatenate([group_speed, a_speed], axis=0)
    south_wet = jnp.concatenate([wet_field, a_wet], axis=0)
    north = propagate(
        jnp.concatenate([b_spec[tile_rows - first_half :], masked[:, :, :half]], axis=0),
        north_speed[tile_rows - first_half :],
        north_wet[tile_rows - first_half :],
        cosines[:half],
        sines[:half],
        True,
        first_half,
    )
    south = propagate(
        jnp.concatenate([masked[:, :, half:], a_spec[:first_half]], axis=0),
        south_speed[: 2 * tile_rows - (tile_rows - first_half)],
        south_wet[: 2 * tile_rows - (tile_rows - first_half)],
        cosines[half:],
        sines[half:],
        False,
        first_half,
    )
    extended = jnp.concatenate([spectrum_halo[-1][0], masked, spectrum_halo[1][0]], axis=1)
    transfer = interaction(extended, masked, quad_offsets, quad_weights)
    known = {0: partial_value, -1: spectrum_halo[-1][1][0], 1: spectrum_halo[1][1][0]}

    second = SUBSTEPS - first_half
    north_mid = from_neighbour(north, "geo", 1)
    south_mid = from_neighbour(south, "geo", -1)
    transfer_halo = tagged_exchange(
        transfer, jnp.stack([known[-1], known[0], known[1]]), "freq", FH
    )
    north_mid, south_mid, transfer_halo = lax.optimization_barrier(
        (north_mid, south_mid, transfer_halo)
    )
    known[-2] = transfer_halo[-1][1][0]
    known[2] = transfer_halo[1][1][2]
    north = propagate(
        jnp.concatenate([north_mid[tile_rows - second :], north], axis=0),
        north_speed[tile_rows - second :],
        north_wet[tile_rows - second :],
        cosines[:half],
        sines[:half],
        True,
        second,
    )
    south = propagate(
        jnp.concatenate([south, south_mid[:second]], axis=0),
        south_speed[: tile_rows + second],
        south_wet[: tile_rows + second],
        cosines[half:],
        sines[half:],
        False,
        second,
    )
    spread = jnp.concatenate([transfer_halo[-1][0], transfer, transfer_halo[1][0]], axis=1)
    change = redistribute(spread, transfer, quad_offsets, quad_weights)

    orbital = jnp.sqrt(gathered_sum(known, freq_index, freq_total, partial_value))
    full_step = SUBSTEPS * sub_step
    damping = 1.0 + full_step * canopy * veg_field * orbital
    increment = (masked + full_step * change) / damping[:, None, None, :] - masked
    moved = jnp.concatenate([north, south], axis=2)
    return (wet_four * (moved + increment), orbital)


def solution(mesh):
    placed = (
        P("geo", "freq", None, None),
        P("geo", None),
        P("geo", None),
        P("geo", None),
        P("geo", None),
        P(),
        P(),
    )
    return jax.shard_map(
        body,
        mesh=mesh,
        in_specs=placed,
        out_specs=(P("geo", "freq", None, None), P("geo", None)),
        check_vma=False,
    )
```

```python
import math

import jax
import jax.numpy as jnp
from jax import lax
from jax.sharding import PartitionSpec as P

FH = 4
SUBSTEPS = 8


gravity = 9.81
base_freq = 0.03
freq_ratio = 1.05
cell_size = 20.0
sub_step = 2.0
coupling = 0.01
coef_plus = 0.4096
coef_minus = 3.1605
coef_both = 2.589


def from_neighbour(block, axis, distance, cyclic=False):
    count = lax.axis_size(axis)
    if cyclic:
        pairs = [(i, (i + distance) % count) for i in range(count)]
    else:
        pairs = [(i, i + distance) for i in range(count) if 0 <= i + distance < count]
    return lax.ppermute(block, axis, pairs)


def halo(block, axis, dim, width, side, cyclic=False):
    size = block.shape[dim]
    parts = []
    distance = 1
    need = width
    while need > 0:
        take = min(size, need)
        if side < 0:
            piece = lax.slice_in_dim(block, size - take, size, axis=dim)
            parts.insert(0, from_neighbour(piece, axis, distance, cyclic))
        else:
            piece = lax.slice_in_dim(block, 0, take, axis=dim)
            parts.append(from_neighbour(piece, axis, -distance, cyclic))
        need -= take
        distance += 1
    return parts


def butterfly_sum(value, axis):
    count = lax.axis_size(axis)
    assert count & (count - 1) == 0
    step = 1
    while step < count:
        value = value + lax.ppermute(value, axis, [(i, i ^ step) for i in range(count)])
        step *= 2
    return value


def gathered_sum(known, index, count, value):
    reach = max(known)
    if count > 2 * (2 * reach + 1) - 2 or count % 2:
        return butterfly_sum(value, "freq")
    far = count // 2
    ordered = jnp.stack([known[o] for o in range(-reach, reach + 1)])
    more = from_neighbour(ordered, "freq", far, True)
    table = []
    for rel in range(count):
        off = rel if rel <= reach else rel - count
        if -reach <= off <= reach:
            table.append(known[off])
        else:
            table.append(more[rel - far + reach])
    table = jnp.stack(table)
    table = jnp.concatenate([table, table], axis=0)
    start = (count - index) % count
    glob = lax.dynamic_slice_in_dim(table, start, count, axis=0)
    while glob.shape[0] > 1:
        glob = glob[0::2] + glob[1::2]
    return glob[0]


def physics(radian_freq, water_depth, dir_count):
    square = (radian_freq * radian_freq)[None, :, None]
    column = water_depth[:, None, :]
    depth_ratio = square * column / gravity
    depth_wave = depth_ratio / jnp.sqrt(jnp.tanh(depth_ratio))
    group_speed = (
        radian_freq[None, :, None]
        * column
        / depth_wave
        * (0.5 + depth_wave / jnp.sinh(2.0 * depth_wave))
    )
    orbit_weight = (
        square
        / jnp.sinh(depth_wave) ** 2
        * (radian_freq * (freq_ratio - 1.0))[None, :, None]
        * (2.0 * math.pi / dir_count)
    )
    return (group_speed, orbit_weight)


def angles_of(dir_count):
    angles = (jnp.arange(dir_count, dtype=jnp.float32) + 0.5) * (2.0 * math.pi / dir_count)
    return (jnp.cos(angles), jnp.sin(angles))


def shifted(doubled, freq_start, dir_off, count):
    dir_count = doubled.shape[2] // 2
    starts = (
        jnp.zeros((), jnp.int32),
        freq_start,
        dir_off % dir_count,
        jnp.zeros((), jnp.int32),
    )
    return lax.dynamic_slice(
        doubled, starts, (doubled.shape[0], count, dir_count, doubled.shape[3])
    )


def source_change(extended, quad_offsets, quad_weights, count):
    up_bins, down_bins, up_turn, down_turn = (
        quad_offsets[0],
        quad_offsets[1],
        quad_offsets[2],
        quad_offsets[3],
    )
    weight_up, weight_down = (quad_weights[0], quad_weights[1])
    wide = count + 2 * FH
    doubled = jnp.concatenate([extended, extended], axis=2)
    centre = lax.slice_in_dim(extended, FH, FH + wide, axis=1)
    upper = weight_up * shifted(doubled, FH + up_bins, up_turn, wide) + (
        1.0 - weight_up
    ) * shifted(doubled, FH + up_bins + 1, up_turn, wide)
    lower = weight_down * shifted(doubled, FH - down_bins, -down_turn, wide) + (
        1.0 - weight_down
    ) * shifted(doubled, FH - down_bins - 1, -down_turn, wide)
    transfer = coupling * (
        centre * centre * (coef_plus * upper + coef_minus * lower)
        - coef_both * centre * upper * lower
    )
    spread = jnp.concatenate([transfer, transfer], axis=2)
    gained = weight_up * shifted(spread, FH - up_bins, -up_turn, count) + (
        1.0 - weight_up
    ) * shifted(spread, FH - up_bins - 1, -up_turn, count)
    gained = (
        gained
        + weight_down * shifted(spread, FH + down_bins, down_turn, count)
        + (1.0 - weight_down) * shifted(spread, FH + down_bins + 1, down_turn, count)
    )
    own = lax.slice_in_dim(transfer, FH, FH + count, axis=1)
    return gained - 2.0 * own


def east_west(east_flux, cosines):
    zeros = jnp.zeros_like(east_flux[..., :1])
    behind = jnp.concatenate([zeros, east_flux[..., :-1]], axis=-1)
    ahead = jnp.concatenate([east_flux[..., 1:], zeros], axis=-1)
    east_going = (cosines > 0.0)[None, None, :, None]
    return jnp.where(east_going, east_flux - behind, ahead - east_flux)


def propagate(spectrum, speed, wet, cosines, sines, northward):
    step_ratio = sub_step / cell_size
    east_speed = speed[:, :, None, :] * cosines[None, None, :, None]
    north_speed = speed[:, :, None, :] * sines[None, None, :, None]
    rows = spectrum.shape[0]
    for substep in range(SUBSTEPS):
        lo, hi = (substep, rows) if northward else (0, rows - substep)
        east_flux = east_speed[lo:hi] * spectrum
        north_flux = north_speed[lo:hi] * spectrum
        along = north_flux[1:] - north_flux[:-1]
        across = east_west(east_flux, cosines)
        if northward:
            spectrum = wet[lo + 1 : hi, None, None, :] * (
                spectrum[1:] - step_ratio * (across[1:] + along)
            )
        else:
            spectrum = wet[lo : hi - 1, None, None, :] * (
                spectrum[:-1] - step_ratio * (across[:-1] + along)
            )
    return spectrum


def body(energy, water_depth, wet_mask, vegetation, canopy, quad_offsets, quad_weights):
    tile_rows, freq_count, dir_count, tile_cols = energy.shape
    wet_field = wet_mask.astype(jnp.float32)
    veg_field = vegetation.astype(jnp.float32)
    wet_four = wet_field[:, None, None, :]
    masked = wet_four * energy
    first_bin = lax.axis_index("freq") * freq_count
    bin_index = (first_bin + jnp.arange(freq_count, dtype=jnp.int32)).astype(jnp.float32)
    radian_freq = 2.0 * math.pi * base_freq * jnp.power(freq_ratio, bin_index)
    half = dir_count // 2
    cosines, sines = angles_of(dir_count)

    fields = jnp.zeros((tile_rows, 1, half, tile_cols), jnp.float32)
    fields = fields.at[:, 0, 0, :].set(wet_field).at[:, 0, 1, :].set(water_depth)
    north_msg = jnp.concatenate([masked[:, :, :half], fields], axis=1)
    south_msg = jnp.concatenate([masked[:, :, half:], fields], axis=1)
    below = halo(north_msg, "geo", 0, SUBSTEPS, -1)
    above = halo(south_msg, "geo", 0, SUBSTEPS, +1)

    group_speed, orbit_weight = physics(radian_freq, water_depth, dir_count)
    partial_value = jnp.sum(orbit_weight * jnp.sum(energy, axis=2), axis=1)

    freq_index = lax.axis_index("freq")
    freq_total = lax.axis_size("freq")
    slot = jnp.zeros((tile_rows, 1, dir_count, tile_cols), jnp.float32)
    slot = slot.at[:, 0, 0, :].set(partial_value)
    gated, slot, below, above = lax.optimization_barrier((masked, slot, below, above))

    def tagged_halo(side):
        pieces = []
        distance = 1
        need = 2 * FH
        while need > 0:
            take = min(freq_count, need)
            lo = freq_count - take if side < 0 else 0
            piece = jnp.concatenate(
                [lax.slice_in_dim(gated, lo, lo + take, axis=1), slot], axis=1
            )
            got = from_neighbour(piece, "freq", -side * distance, True)
            source = freq_index + side * distance
            inside = (source >= 0) & (source < freq_total)
            pieces.append(
                (distance * side, jnp.where(inside, got[:, :take], 0.0), got[:, take, 0, :])
            )
            need -= take
            distance += 1
        return pieces

    low = tagged_halo(-1)
    high = tagged_halo(+1)
    geo_index = lax.axis_index("geo")
    geo_count = lax.axis_size("geo")

    def unpack(parts, offsets):
        spectra, speeds, wets = [], [], []
        for part, offset in zip(parts, offsets):
            valid = (geo_index + offset >= 0) & (geo_index + offset < geo_count)
            depth = jnp.where(valid, part[:, freq_count, 1, :], 1.0)
            spectra.append(part[:, :freq_count])
            wets.append(part[:, freq_count, 0, :])
            speeds.append(physics(radian_freq, depth, dir_count)[0])
        return spectra, speeds, wets

    n_off = [-(len(below) - k) for k in range(len(below))]
    b_spec, b_speed, b_wet = unpack(below, n_off)
    north = propagate(
        jnp.concatenate(b_spec + [masked[:, :, :half]], axis=0),
        jnp.concatenate(b_speed + [group_speed], axis=0),
        jnp.concatenate(b_wet + [wet_field], axis=0),
        cosines[:half],
        sines[:half],
        True,
    )
    arrays = [(p[1], p[2]) for p in low + high]
    north, arrays = lax.optimization_barrier((north, arrays))
    tagged = [(p[0],) + tuple(a) for p, a in zip(low + high, arrays)]
    low, high = tagged[: len(low)], tagged[len(low) :]
    low_bins = [p[1] for p in reversed(low)]
    high_bins = [p[1] for p in high]
    known = {0: partial_value}
    for offset, _, value in low + high:
        known[offset] = value
    orbital = jnp.sqrt(gathered_sum(known, freq_index, freq_total, partial_value))
    full_step = SUBSTEPS * sub_step
    damping = 1.0 + full_step * canopy * veg_field * orbital

    extended = jnp.concatenate(low_bins + [masked] + high_bins, axis=1)
    change = source_change(extended, quad_offsets, quad_weights, freq_count)
    increment = (masked + full_step * change) / damping[:, None, None, :] - masked

    s_off = [k + 1 for k in range(len(above))]
    a_spec, a_speed, a_wet = unpack(above, s_off)
    south = propagate(
        jnp.concatenate([masked[:, :, half:]] + a_spec, axis=0),
        jnp.concatenate([group_speed] + a_speed, axis=0),
        jnp.concatenate([wet_field] + a_wet, axis=0),
        cosines[half:],
        sines[half:],
        False,
    )
    moved = jnp.concatenate([north, south], axis=2)
    return (wet_four * (moved + increment), orbital)


def solution(mesh):
    placed = (
        P("geo", "freq", None, None),
        P("geo", None),
        P("geo", None),
        P("geo", None),
        P("geo", None),
        P(),
        P(),
    )
    return jax.shard_map(
        body,
        mesh=mesh,
        in_specs=placed,
        out_specs=(P("geo", "freq", None, None), P("geo", None)),
        check_vma=False,
    )
```

```python
import math

import jax
import jax.numpy as jnp
from jax import lax
from jax.sharding import PartitionSpec as P

FH = 4
SUBSTEPS = 8


gravity = 9.81
base_freq = 0.03
freq_ratio = 1.05
cell_size = 20.0
sub_step = 2.0
coupling = 0.01
coef_plus = 0.4096
coef_minus = 3.1605
coef_both = 2.589


def from_neighbour(block, axis, distance, cyclic=False):
    count = lax.axis_size(axis)
    if cyclic:
        pairs = [(i, (i + distance) % count) for i in range(count)]
    else:
        pairs = [(i, i + distance) for i in range(count) if 0 <= i + distance < count]
    return lax.ppermute(block, axis, pairs)


def halo(block, axis, dim, width, side, cyclic=False):
    size = block.shape[dim]
    parts = []
    distance = 1
    need = width
    while need > 0:
        take = min(size, need)
        if side < 0:
            piece = lax.slice_in_dim(block, size - take, size, axis=dim)
            parts.insert(0, from_neighbour(piece, axis, distance, cyclic))
        else:
            piece = lax.slice_in_dim(block, 0, take, axis=dim)
            parts.append(from_neighbour(piece, axis, -distance, cyclic))
        need -= take
        distance += 1
    return parts


def butterfly_sum(value, axis):
    count = lax.axis_size(axis)
    assert count & (count - 1) == 0
    step = 1
    while step < count:
        value = value + lax.ppermute(value, axis, [(i, i ^ step) for i in range(count)])
        step *= 2
    return value


def gathered_sum(known, index, count, value):
    reach = max(known)
    if count > 2 * (2 * reach + 1) - 2 or count % 2:
        return butterfly_sum(value, "freq")
    far = count // 2
    ordered = jnp.stack([known[o] for o in range(-reach, reach + 1)])
    more = from_neighbour(ordered, "freq", far, True)
    table = []
    for rel in range(count):
        off = rel if rel <= reach else rel - count
        if -reach <= off <= reach:
            table.append(known[off])
        else:
            table.append(more[rel - far + reach])
    table = jnp.stack(table)
    table = jnp.concatenate([table, table], axis=0)
    start = (count - index) % count
    glob = lax.dynamic_slice_in_dim(table, start, count, axis=0)
    while glob.shape[0] > 1:
        glob = glob[0::2] + glob[1::2]
    return glob[0]


def full_sum(known, index, count, value):
    if len(known) < count or count % 2:
        return butterfly_sum(value, "freq")
    table = jnp.stack([known[rel] for rel in range(count)])
    table = jnp.concatenate([table, table], axis=0)
    glob = lax.dynamic_slice_in_dim(table, (count - index) % count, count, axis=0)
    while glob.shape[0] > 1:
        glob = glob[0::2] + glob[1::2]
    return glob[0]


def physics(radian_freq, water_depth, dir_count):
    square = (radian_freq * radian_freq)[None, :, None]
    column = water_depth[:, None, :]
    depth_ratio = square * column / gravity
    depth_wave = depth_ratio / jnp.sqrt(jnp.tanh(depth_ratio))
    group_speed = (
        radian_freq[None, :, None]
        * column
        / depth_wave
        * (0.5 + depth_wave / jnp.sinh(2.0 * depth_wave))
    )
    orbit_weight = (
        square
        / jnp.sinh(depth_wave) ** 2
        * (radian_freq * (freq_ratio - 1.0))[None, :, None]
        * (2.0 * math.pi / dir_count)
    )
    return (group_speed, orbit_weight)


def angles_of(dir_count):
    angles = (jnp.arange(dir_count, dtype=jnp.float32) + 0.5) * (2.0 * math.pi / dir_count)
    return (jnp.cos(angles), jnp.sin(angles))


def shifted(doubled, freq_start, dir_off, count):
    dir_count = doubled.shape[2] // 2
    starts = (
        jnp.zeros((), jnp.int32),
        freq_start,
        dir_off % dir_count,
        jnp.zeros((), jnp.int32),
    )
    return lax.dynamic_slice(
        doubled, starts, (doubled.shape[0], count, dir_count, doubled.shape[3])
    )


def source_change(extended, quad_offsets, quad_weights, count):
    up_bins, down_bins, up_turn, down_turn = (
        quad_offsets[0],
        quad_offsets[1],
        quad_offsets[2],
        quad_offsets[3],
    )
    weight_up, weight_down = (quad_weights[0], quad_weights[1])
    wide = count + 2 * FH
    doubled = jnp.concatenate([extended, extended], axis=2)
    centre = lax.slice_in_dim(extended, FH, FH + wide, axis=1)
    upper = weight_up * shifted(doubled, FH + up_bins, up_turn, wide) + (
        1.0 - weight_up
    ) * shifted(doubled, FH + up_bins + 1, up_turn, wide)
    lower = weight_down * shifted(doubled, FH - down_bins, -down_turn, wide) + (
        1.0 - weight_down
    ) * shifted(doubled, FH - down_bins - 1, -down_turn, wide)
    transfer = coupling * (
        centre * centre * (coef_plus * upper + coef_minus * lower)
        - coef_both * centre * upper * lower
    )
    spread = jnp.concatenate([transfer, transfer], axis=2)
    gained = weight_up * shifted(spread, FH - up_bins, -up_turn, count) + (
        1.0 - weight_up
    ) * shifted(spread, FH - up_bins - 1, -up_turn, count)
    gained = (
        gained
        + weight_down * shifted(spread, FH + down_bins, down_turn, count)
        + (1.0 - weight_down) * shifted(spread, FH + down_bins + 1, down_turn, count)
    )
    own = lax.slice_in_dim(transfer, FH, FH + count, axis=1)
    return gained - 2.0 * own


def east_west(east_flux, cosines):
    zeros = jnp.zeros_like(east_flux[..., :1])
    behind = jnp.concatenate([zeros, east_flux[..., :-1]], axis=-1)
    ahead = jnp.concatenate([east_flux[..., 1:], zeros], axis=-1)
    east_going = (cosines > 0.0)[None, None, :, None]
    return jnp.where(east_going, east_flux - behind, ahead - east_flux)


def propagate(spectrum, speed, wet, cosines, sines, northward):
    step_ratio = sub_step / cell_size
    east_speed = speed[:, :, None, :] * cosines[None, None, :, None]
    north_speed = speed[:, :, None, :] * sines[None, None, :, None]
    rows = spectrum.shape[0]
    for substep in range(SUBSTEPS):
        lo, hi = (substep, rows) if northward else (0, rows - substep)
        east_flux = east_speed[lo:hi] * spectrum
        north_flux = north_speed[lo:hi] * spectrum
        along = north_flux[1:] - north_flux[:-1]
        across = east_west(east_flux, cosines)
        if northward:
            spectrum = wet[lo + 1 : hi, None, None, :] * (
                spectrum[1:] - step_ratio * (across[1:] + along)
            )
        else:
            spectrum = wet[lo : hi - 1, None, None, :] * (
                spectrum[:-1] - step_ratio * (across[:-1] + along)
            )
    return spectrum


def body(energy, water_depth, wet_mask, vegetation, canopy, quad_offsets, quad_weights):
    tile_rows, freq_count, dir_count, tile_cols = energy.shape
    wet_field = wet_mask.astype(jnp.float32)
    veg_field = vegetation.astype(jnp.float32)
    wet_four = wet_field[:, None, None, :]
    masked = wet_four * energy
    first_bin = lax.axis_index("freq") * freq_count
    bin_index = (first_bin + jnp.arange(freq_count, dtype=jnp.int32)).astype(jnp.float32)
    radian_freq = 2.0 * math.pi * base_freq * jnp.power(freq_ratio, bin_index)
    half = dir_count // 2
    cosines, sines = angles_of(dir_count)

    fields = jnp.zeros((tile_rows, 1, half, tile_cols), jnp.float32)
    fields = fields.at[:, 0, 0, :].set(wet_field).at[:, 0, 1, :].set(water_depth)
    north_msg = jnp.concatenate([masked[:, :, :half], fields], axis=1)
    south_msg = jnp.concatenate([masked[:, :, half:], fields], axis=1)
    below = halo(north_msg, "geo", 0, SUBSTEPS, -1)
    above = halo(south_msg, "geo", 0, SUBSTEPS, +1)

    group_speed, orbit_weight = physics(radian_freq, water_depth, dir_count)
    partial_value = jnp.sum(orbit_weight * jnp.sum(energy, axis=2), axis=1)

    freq_index = lax.axis_index("freq")
    freq_total = lax.axis_size("freq")
    slot = jnp.zeros((tile_rows, 1, dir_count, tile_cols), jnp.float32)
    far = freq_total // 2
    opposite = from_neighbour(partial_value, "freq", far, True)
    slot = slot.at[:, 0, 0, :].set(partial_value).at[:, 0, 1, :].set(opposite)
    gated, slot, below, above, opposite = lax.optimization_barrier(
        (masked, slot, below, above, opposite)
    )

    def tagged_halo(side):
        pieces = []
        distance = 1
        need = 2 * FH
        while need > 0:
            take = min(freq_count, need)
            lo = freq_count - take if side < 0 else 0
            piece = jnp.concatenate(
                [lax.slice_in_dim(gated, lo, lo + take, axis=1), slot], axis=1
            )
            got = from_neighbour(piece, "freq", -side * distance, True)
            source = freq_index + side * distance
            inside = (source >= 0) & (source < freq_total)
            pieces.append(
                (distance * side, jnp.where(inside, got[:, :take], 0.0), got[:, take, :2, :])
            )
            need -= take
            distance += 1
        return pieces

    low = tagged_halo(-1)
    high = tagged_halo(+1)
    geo_index = lax.axis_index("geo")
    geo_count = lax.axis_size("geo")

    def unpack(parts, offsets):
        spectra, speeds, wets = [], [], []
        for part, offset in zip(parts, offsets):
            valid = (geo_index + offset >= 0) & (geo_index + offset < geo_count)
            depth = jnp.where(valid, part[:, freq_count, 1, :], 1.0)
            spectra.append(part[:, :freq_count])
            wets.append(part[:, freq_count, 0, :])
            speeds.append(physics(radian_freq, depth, dir_count)[0])
        return spectra, speeds, wets

    n_off = [-(len(below) - k) for k in range(len(below))]
    b_spec, b_speed, b_wet = unpack(below, n_off)
    north = propagate(
        jnp.concatenate(b_spec + [masked[:, :, :half]], axis=0),
        jnp.concatenate(b_speed + [group_speed], axis=0),
        jnp.concatenate(b_wet + [wet_field], axis=0),
        cosines[:half],
        sines[:half],
        True,
    )
    arrays = [(p[1], p[2]) for p in low + high]
    north, arrays = lax.optimization_barrier((north, arrays))
    tagged = [(p[0],) + tuple(a) for p, a in zip(low + high, arrays)]
    low, high = tagged[: len(low)], tagged[len(low) :]
    low_bins = [p[1] for p in reversed(low)]
    high_bins = [p[1] for p in high]
    known = {0: partial_value, far: opposite}
    for offset, _, value in low + high:
        known[offset % freq_total] = value[:, 0]
        known[(offset + far) % freq_total] = value[:, 1]
    orbital = jnp.sqrt(full_sum(known, freq_index, freq_total, partial_value))
    full_step = SUBSTEPS * sub_step
    damping = 1.0 + full_step * canopy * veg_field * orbital

    extended = jnp.concatenate(low_bins + [masked] + high_bins, axis=1)
    change = source_change(extended, quad_offsets, quad_weights, freq_count)
    increment = (masked + full_step * change) / damping[:, None, None, :] - masked

    s_off = [k + 1 for k in range(len(above))]
    a_spec, a_speed, a_wet = unpack(above, s_off)
    south = propagate(
        jnp.concatenate([masked[:, :, half:]] + a_spec, axis=0),
        jnp.concatenate([group_speed] + a_speed, axis=0),
        jnp.concatenate([wet_field] + a_wet, axis=0),
        cosines[half:],
        sines[half:],
        False,
    )
    moved = jnp.concatenate([north, south], axis=2)
    return (wet_four * (moved + increment), orbital)


def solution(mesh):
    placed = (
        P("geo", "freq", None, None),
        P("geo", None),
        P("geo", None),
        P("geo", None),
        P("geo", None),
        P(),
        P(),
    )
    return jax.shard_map(
        body,
        mesh=mesh,
        in_specs=placed,
        out_specs=(P("geo", "freq", None, None), P("geo", None)),
        check_vma=False,
    )
```

```python
import math

import jax
import jax.numpy as jnp
from jax import lax
from jax.sharding import PartitionSpec as P

FH = 4
SUBSTEPS = 8


gravity = 9.81
base_freq = 0.03
freq_ratio = 1.05
cell_size = 20.0
sub_step = 2.0
coupling = 0.01
coef_plus = 0.4096
coef_minus = 3.1605
coef_both = 2.589


def from_neighbour(block, axis, distance, cyclic=False):
    count = lax.axis_size(axis)
    if cyclic:
        pairs = [(i, (i + distance) % count) for i in range(count)]
    else:
        pairs = [(i, i + distance) for i in range(count) if 0 <= i + distance < count]
    return lax.ppermute(block, axis, pairs)


def halo(block, axis, dim, width, side, cyclic=False):
    size = block.shape[dim]
    parts = []
    distance = 1
    need = width
    while need > 0:
        take = min(size, need)
        if side < 0:
            piece = lax.slice_in_dim(block, size - take, size, axis=dim)
            parts.insert(0, from_neighbour(piece, axis, distance, cyclic))
        else:
            piece = lax.slice_in_dim(block, 0, take, axis=dim)
            parts.append(from_neighbour(piece, axis, -distance, cyclic))
        need -= take
        distance += 1
    return parts


def butterfly_sum(value, axis):
    count = lax.axis_size(axis)
    assert count & (count - 1) == 0
    step = 1
    while step < count:
        value = value + lax.ppermute(value, axis, [(i, i ^ step) for i in range(count)])
        step *= 2
    return value


def gathered_sum(known, index, count, value):
    reach = max(known)
    if count > 2 * (2 * reach + 1) - 2 or count % 2:
        return butterfly_sum(value, "freq")
    far = count // 2
    ordered = jnp.stack([known[o] for o in range(-reach, reach + 1)])
    more = from_neighbour(ordered, "freq", far, True)
    table = []
    for rel in range(count):
        off = rel if rel <= reach else rel - count
        if -reach <= off <= reach:
            table.append(known[off])
        else:
            table.append(more[rel - far + reach])
    table = jnp.stack(table)
    table = jnp.concatenate([table, table], axis=0)
    start = (count - index) % count
    glob = lax.dynamic_slice_in_dim(table, start, count, axis=0)
    while glob.shape[0] > 1:
        glob = glob[0::2] + glob[1::2]
    return glob[0]


def full_sum(known, index, count, value):
    if len(known) < count or count % 2:
        return butterfly_sum(value, "freq")
    table = jnp.stack([known[rel] for rel in range(count)])
    table = jnp.concatenate([table, table], axis=0)
    glob = lax.dynamic_slice_in_dim(table, (count - index) % count, count, axis=0)
    while glob.shape[0] > 1:
        glob = glob[0::2] + glob[1::2]
    return glob[0]


def physics(radian_freq, water_depth, dir_count):
    square = (radian_freq * radian_freq)[None, :, None]
    column = water_depth[:, None, :]
    depth_ratio = square * column / gravity
    depth_wave = depth_ratio / jnp.sqrt(jnp.tanh(depth_ratio))
    group_speed = (
        radian_freq[None, :, None]
        * column
        / depth_wave
        * (0.5 + depth_wave / jnp.sinh(2.0 * depth_wave))
    )
    orbit_weight = (
        square
        / jnp.sinh(depth_wave) ** 2
        * (radian_freq * (freq_ratio - 1.0))[None, :, None]
        * (2.0 * math.pi / dir_count)
    )
    return (group_speed, orbit_weight)


def angles_of(dir_count):
    angles = (jnp.arange(dir_count, dtype=jnp.float32) + 0.5) * (2.0 * math.pi / dir_count)
    return (jnp.cos(angles), jnp.sin(angles))


def shifted(doubled, freq_start, dir_off, count):
    dir_count = doubled.shape[2] // 2
    starts = (
        jnp.zeros((), jnp.int32),
        freq_start,
        dir_off % dir_count,
        jnp.zeros((), jnp.int32),
    )
    return lax.dynamic_slice(
        doubled, starts, (doubled.shape[0], count, dir_count, doubled.shape[3])
    )


def source_change(extended, quad_offsets, quad_weights, count):
    up_bins, down_bins, up_turn, down_turn = (
        quad_offsets[0],
        quad_offsets[1],
        quad_offsets[2],
        quad_offsets[3],
    )
    weight_up, weight_down = (quad_weights[0], quad_weights[1])
    wide = count + 2 * FH
    doubled = jnp.concatenate([extended, extended], axis=2)
    centre = lax.slice_in_dim(extended, FH, FH + wide, axis=1)
    upper = weight_up * shifted(doubled, FH + up_bins, up_turn, wide) + (
        1.0 - weight_up
    ) * shifted(doubled, FH + up_bins + 1, up_turn, wide)
    lower = weight_down * shifted(doubled, FH - down_bins, -down_turn, wide) + (
        1.0 - weight_down
    ) * shifted(doubled, FH - down_bins - 1, -down_turn, wide)
    transfer = coupling * (
        centre * centre * (coef_plus * upper + coef_minus * lower)
        - coef_both * centre * upper * lower
    )
    spread = jnp.concatenate([transfer, transfer], axis=2)
    gained = weight_up * shifted(spread, FH - up_bins, -up_turn, count) + (
        1.0 - weight_up
    ) * shifted(spread, FH - up_bins - 1, -up_turn, count)
    gained = (
        gained
        + weight_down * shifted(spread, FH + down_bins, down_turn, count)
        + (1.0 - weight_down) * shifted(spread, FH + down_bins + 1, down_turn, count)
    )
    own = lax.slice_in_dim(transfer, FH, FH + count, axis=1)
    return gained - 2.0 * own


def east_west(east_flux, cosines):
    zeros = jnp.zeros_like(east_flux[..., :1])
    behind = jnp.concatenate([zeros, east_flux[..., :-1]], axis=-1)
    ahead = jnp.concatenate([east_flux[..., 1:], zeros], axis=-1)
    east_going = (cosines > 0.0)[None, None, :, None]
    return jnp.where(east_going, east_flux - behind, ahead - east_flux)


def propagate(spectrum, speed, wet, cosines, sines, northward):
    step_ratio = sub_step / cell_size
    east_speed = speed[:, :, None, :] * cosines[None, None, :, None]
    north_speed = speed[:, :, None, :] * sines[None, None, :, None]
    rows = spectrum.shape[0]
    for substep in range(SUBSTEPS):
        lo, hi = (substep, rows) if northward else (0, rows - substep)
        east_flux = east_speed[lo:hi] * spectrum
        north_flux = north_speed[lo:hi] * spectrum
        along = north_flux[1:] - north_flux[:-1]
        across = east_west(east_flux, cosines)
        if northward:
            spectrum = wet[lo + 1 : hi, None, None, :] * (
                spectrum[1:] - step_ratio * (across[1:] + along)
            )
        else:
            spectrum = wet[lo : hi - 1, None, None, :] * (
                spectrum[:-1] - step_ratio * (across[:-1] + along)
            )
    return spectrum


def body(energy, water_depth, wet_mask, vegetation, canopy, quad_offsets, quad_weights):
    tile_rows, freq_count, dir_count, tile_cols = energy.shape
    wet_field = wet_mask.astype(jnp.float32)
    veg_field = vegetation.astype(jnp.float32)
    wet_four = wet_field[:, None, None, :]
    masked = wet_four * energy
    first_bin = lax.axis_index("freq") * freq_count
    bin_index = (first_bin + jnp.arange(freq_count, dtype=jnp.int32)).astype(jnp.float32)
    radian_freq = 2.0 * math.pi * base_freq * jnp.power(freq_ratio, bin_index)
    half = dir_count // 2
    cosines, sines = angles_of(dir_count)

    fields = jnp.zeros((tile_rows, 1, half, tile_cols), jnp.float32)
    fields = fields.at[:, 0, 0, :].set(wet_field).at[:, 0, 1, :].set(water_depth)
    north_msg = jnp.concatenate([masked[:, :, :half], fields], axis=1)
    south_msg = jnp.concatenate([masked[:, :, half:], fields], axis=1)
    below = halo(north_msg, "geo", 0, SUBSTEPS, -1)
    above = halo(south_msg, "geo", 0, SUBSTEPS, +1)

    group_speed, orbit_weight = physics(radian_freq, water_depth, dir_count)
    partial_value = jnp.sum(orbit_weight * jnp.sum(energy, axis=2), axis=1)

    freq_index = lax.axis_index("freq")
    freq_total = lax.axis_size("freq")
    slot = jnp.zeros((tile_rows, 1, dir_count, tile_cols), jnp.float32)
    far = freq_total // 2
    opposite = from_neighbour(partial_value, "freq", far, True)
    slot = slot.at[:, 0, 0, :].set(partial_value).at[:, 0, 1, :].set(opposite)
    gated, slot, below, above, opposite = lax.optimization_barrier(
        (masked, slot, below, above, opposite)
    )

    def tagged_halo(side):
        pieces = []
        distance = 1
        need = 2 * FH
        while need > 0:
            take = min(freq_count, need)
            lo = freq_count - take if side < 0 else 0
            got = from_neighbour(jnp.concatenate([gated, slot], axis=1), "freq", -side * distance, True)
            source = freq_index + side * distance
            inside = (source >= 0) & (source < freq_total)
            pieces.append(
                (
                    distance * side,
                    jnp.where(inside, got[:, lo : lo + take], 0.0),
                    got[:, freq_count, :2, :],
                )
            )
            need -= take
            distance += 1
        return pieces

    low = tagged_halo(-1)
    high = tagged_halo(+1)
    geo_index = lax.axis_index("geo")
    geo_count = lax.axis_size("geo")

    def unpack(parts, offsets):
        spectra, speeds, wets = [], [], []
        for part, offset in zip(parts, offsets):
            valid = (geo_index + offset >= 0) & (geo_index + offset < geo_count)
            depth = jnp.where(valid, part[:, freq_count, 1, :], 1.0)
            spectra.append(part[:, :freq_count])
            wets.append(part[:, freq_count, 0, :])
            speeds.append(physics(radian_freq, depth, dir_count)[0])
        return spectra, speeds, wets

    n_off = [-(len(below) - k) for k in range(len(below))]
    b_spec, b_speed, b_wet = unpack(below, n_off)
    north = propagate(
        jnp.concatenate(b_spec + [masked[:, :, :half]], axis=0),
        jnp.concatenate(b_speed + [group_speed], axis=0),
        jnp.concatenate(b_wet + [wet_field], axis=0),
        cosines[:half],
        sines[:half],
        True,
    )
    arrays = [(p[1], p[2]) for p in low + high]
    north, arrays = lax.optimization_barrier((north, arrays))
    tagged = [(p[0],) + tuple(a) for p, a in zip(low + high, arrays)]
    low, high = tagged[: len(low)], tagged[len(low) :]
    low_bins = [p[1] for p in reversed(low)]
    high_bins = [p[1] for p in high]
    known = {0: partial_value, far: opposite}
    for offset, _, value in low + high:
        known[offset % freq_total] = value[:, 0]
        known[(offset + far) % freq_total] = value[:, 1]
    orbital = jnp.sqrt(full_sum(known, freq_index, freq_total, partial_value))
    full_step = SUBSTEPS * sub_step
    damping = 1.0 + full_step * canopy * veg_field * orbital

    extended = jnp.concatenate(low_bins + [masked] + high_bins, axis=1)
    change = source_change(extended, quad_offsets, quad_weights, freq_count)
    increment = (masked + full_step * change) / damping[:, None, None, :] - masked

    s_off = [k + 1 for k in range(len(above))]
    a_spec, a_speed, a_wet = unpack(above, s_off)
    south = propagate(
        jnp.concatenate([masked[:, :, half:]] + a_spec, axis=0),
        jnp.concatenate([group_speed] + a_speed, axis=0),
        jnp.concatenate([wet_field] + a_wet, axis=0),
        cosines[half:],
        sines[half:],
        False,
    )
    moved = jnp.concatenate([north, south], axis=2)
    return (wet_four * (moved + increment), orbital)


def solution(mesh):
    placed = (
        P("geo", "freq", None, None),
        P("geo", None),
        P("geo", None),
        P("geo", None),
        P("geo", None),
        P(),
        P(),
    )
    return jax.shard_map(
        body,
        mesh=mesh,
        in_specs=placed,
        out_specs=(P("geo", "freq", None, None), P("geo", None)),
        check_vma=False,
    )
```

```python
import math

import jax
import jax.numpy as jnp
from jax import lax
from jax.sharding import PartitionSpec as P

FH = 4
SUBSTEPS = 8
SEND_BINS = 6


gravity = 9.81
base_freq = 0.03
freq_ratio = 1.05
cell_size = 20.0
sub_step = 2.0
coupling = 0.01
coef_plus = 0.4096
coef_minus = 3.1605
coef_both = 2.589


def from_neighbour(block, axis, distance, cyclic=False):
    count = lax.axis_size(axis)
    if cyclic:
        pairs = [(i, (i + distance) % count) for i in range(count)]
    else:
        pairs = [(i, i + distance) for i in range(count) if 0 <= i + distance < count]
    return lax.ppermute(block, axis, pairs)


def halo(block, axis, dim, width, side, cyclic=False):
    size = block.shape[dim]
    parts = []
    distance = 1
    need = width
    while need > 0:
        take = min(size, need)
        if side < 0:
            piece = lax.slice_in_dim(block, size - take, size, axis=dim)
            parts.insert(0, from_neighbour(piece, axis, distance, cyclic))
        else:
            piece = lax.slice_in_dim(block, 0, take, axis=dim)
            parts.append(from_neighbour(piece, axis, -distance, cyclic))
        need -= take
        distance += 1
    return parts


def butterfly_sum(value, axis):
    count = lax.axis_size(axis)
    assert count & (count - 1) == 0
    step = 1
    while step < count:
        value = value + lax.ppermute(value, axis, [(i, i ^ step) for i in range(count)])
        step *= 2
    return value


def gathered_sum(known, index, count, value):
    reach = max(known)
    if count > 2 * (2 * reach + 1) - 2 or count % 2:
        return butterfly_sum(value, "freq")
    far = count // 2
    ordered = jnp.stack([known[o] for o in range(-reach, reach + 1)])
    more = from_neighbour(ordered, "freq", far, True)
    table = []
    for rel in range(count):
        off = rel if rel <= reach else rel - count
        if -reach <= off <= reach:
            table.append(known[off])
        else:
            table.append(more[rel - far + reach])
    table = jnp.stack(table)
    table = jnp.concatenate([table, table], axis=0)
    start = (count - index) % count
    glob = lax.dynamic_slice_in_dim(table, start, count, axis=0)
    while glob.shape[0] > 1:
        glob = glob[0::2] + glob[1::2]
    return glob[0]


def full_sum(known, index, count, value):
    if len(known) < count or count % 2:
        return butterfly_sum(value, "freq")
    table = jnp.stack([known[rel] for rel in range(count)])
    table = jnp.concatenate([table, table], axis=0)
    glob = lax.dynamic_slice_in_dim(table, (count - index) % count, count, axis=0)
    while glob.shape[0] > 1:
        glob = glob[0::2] + glob[1::2]
    return glob[0]


def physics(radian_freq, water_depth, dir_count):
    square = (radian_freq * radian_freq)[None, :, None]
    column = water_depth[:, None, :]
    depth_ratio = square * column / gravity
    depth_wave = depth_ratio / jnp.sqrt(jnp.tanh(depth_ratio))
    group_speed = (
        radian_freq[None, :, None]
        * column
        / depth_wave
        * (0.5 + depth_wave / jnp.sinh(2.0 * depth_wave))
    )
    orbit_weight = (
        square
        / jnp.sinh(depth_wave) ** 2
        * (radian_freq * (freq_ratio - 1.0))[None, :, None]
        * (2.0 * math.pi / dir_count)
    )
    return (group_speed, orbit_weight)


def angles_of(dir_count):
    angles = (jnp.arange(dir_count, dtype=jnp.float32) + 0.5) * (2.0 * math.pi / dir_count)
    return (jnp.cos(angles), jnp.sin(angles))


def shifted(doubled, freq_start, dir_off, count):
    dir_count = doubled.shape[2] // 2
    starts = (
        jnp.zeros((), jnp.int32),
        freq_start,
        dir_off % dir_count,
        jnp.zeros((), jnp.int32),
    )
    return lax.dynamic_slice(
        doubled, starts, (doubled.shape[0], count, dir_count, doubled.shape[3])
    )


def source_change(extended, quad_offsets, quad_weights, count):
    up_bins, down_bins, up_turn, down_turn = (
        quad_offsets[0],
        quad_offsets[1],
        quad_offsets[2],
        quad_offsets[3],
    )
    weight_up, weight_down = (quad_weights[0], quad_weights[1])
    wide = count + 2 * FH
    doubled = jnp.concatenate([extended, extended], axis=2)
    centre = lax.slice_in_dim(extended, FH, FH + wide, axis=1)
    upper = weight_up * shifted(doubled, FH + up_bins, up_turn, wide) + (
        1.0 - weight_up
    ) * shifted(doubled, FH + up_bins + 1, up_turn, wide)
    lower = weight_down * shifted(doubled, FH - down_bins, -down_turn, wide) + (
        1.0 - weight_down
    ) * shifted(doubled, FH - down_bins - 1, -down_turn, wide)
    transfer = coupling * (
        centre * centre * (coef_plus * upper + coef_minus * lower)
        - coef_both * centre * upper * lower
    )
    spread = jnp.concatenate([transfer, transfer], axis=2)
    gained = weight_up * shifted(spread, FH - up_bins, -up_turn, count) + (
        1.0 - weight_up
    ) * shifted(spread, FH - up_bins - 1, -up_turn, count)
    gained = (
        gained
        + weight_down * shifted(spread, FH + down_bins, down_turn, count)
        + (1.0 - weight_down) * shifted(spread, FH + down_bins + 1, down_turn, count)
    )
    own = lax.slice_in_dim(transfer, FH, FH + count, axis=1)
    return gained - 2.0 * own


def east_west(east_flux, cosines):
    zeros = jnp.zeros_like(east_flux[..., :1])
    behind = jnp.concatenate([zeros, east_flux[..., :-1]], axis=-1)
    ahead = jnp.concatenate([east_flux[..., 1:], zeros], axis=-1)
    east_going = (cosines > 0.0)[None, None, :, None]
    return jnp.where(east_going, east_flux - behind, ahead - east_flux)


def propagate(spectrum, speed, wet, cosines, sines, northward):
    step_ratio = sub_step / cell_size
    east_speed = speed[:, :, None, :] * cosines[None, None, :, None]
    north_speed = speed[:, :, None, :] * sines[None, None, :, None]
    rows = spectrum.shape[0]
    for substep in range(SUBSTEPS):
        lo, hi = (substep, rows) if northward else (0, rows - substep)
        east_flux = east_speed[lo:hi] * spectrum
        north_flux = north_speed[lo:hi] * spectrum
        along = north_flux[1:] - north_flux[:-1]
        across = east_west(east_flux, cosines)
        if northward:
            spectrum = wet[lo + 1 : hi, None, None, :] * (
                spectrum[1:] - step_ratio * (across[1:] + along)
            )
        else:
            spectrum = wet[lo : hi - 1, None, None, :] * (
                spectrum[:-1] - step_ratio * (across[:-1] + along)
            )
    return spectrum


def body(energy, water_depth, wet_mask, vegetation, canopy, quad_offsets, quad_weights):
    tile_rows, freq_count, dir_count, tile_cols = energy.shape
    wet_field = wet_mask.astype(jnp.float32)
    veg_field = vegetation.astype(jnp.float32)
    wet_four = wet_field[:, None, None, :]
    masked = wet_four * energy
    first_bin = lax.axis_index("freq") * freq_count
    bin_index = (first_bin + jnp.arange(freq_count, dtype=jnp.int32)).astype(jnp.float32)
    radian_freq = 2.0 * math.pi * base_freq * jnp.power(freq_ratio, bin_index)
    half = dir_count // 2
    cosines, sines = angles_of(dir_count)

    fields = jnp.stack([wet_field, water_depth], axis=1)
    flat = freq_count * half
    north_msg = jnp.concatenate(
        [masked[:, :, :half].reshape(tile_rows, flat, tile_cols), fields], axis=1
    )
    south_msg = jnp.concatenate(
        [masked[:, :, half:].reshape(tile_rows, flat, tile_cols), fields], axis=1
    )
    below = halo(north_msg, "geo", 0, SUBSTEPS, -1)
    above = halo(south_msg, "geo", 0, SUBSTEPS, +1)

    group_speed, orbit_weight = physics(radian_freq, water_depth, dir_count)
    partial_value = jnp.sum(orbit_weight * jnp.sum(energy, axis=2), axis=1)

    freq_index = lax.axis_index("freq")
    freq_total = lax.axis_size("freq")
    far = freq_total // 2
    opposite = from_neighbour(partial_value, "freq", far, True)
    slot = jnp.stack([partial_value, opposite], axis=1)
    gated, slot, below, above, opposite = lax.optimization_barrier(
        (masked, slot, below, above, opposite)
    )

    def tagged_halo(side):
        pieces = []
        distance = 1
        need = 2 * FH
        while need > 0:
            take = min(freq_count, need)
            send = min(freq_count, max(take, SEND_BINS))
            lo = freq_count - send if side < 0 else 0
            cell = send * dir_count
            block = lax.slice_in_dim(gated, lo, lo + send, axis=1)
            got = from_neighbour(
                jnp.concatenate([block.reshape(tile_rows, cell, tile_cols), slot], axis=1),
                "freq",
                -side * distance,
                True,
            )
            first = send - take if side < 0 else 0
            source = freq_index + side * distance
            inside = (source >= 0) & (source < freq_total)
            bins = got[:, :cell].reshape(tile_rows, send, dir_count, tile_cols)
            pieces.append(
                (
                    distance * side,
                    jnp.where(inside, bins[:, first : first + take], 0.0),
                    got[:, cell:],
                )
            )
            need -= take
            distance += 1
        return pieces

    low = tagged_halo(-1)
    high = tagged_halo(+1)
    geo_index = lax.axis_index("geo")
    geo_count = lax.axis_size("geo")

    def unpack(parts, offsets):
        spectra, speeds, wets = [], [], []
        for part, offset in zip(parts, offsets):
            valid = (geo_index + offset >= 0) & (geo_index + offset < geo_count)
            depth = jnp.where(valid, part[:, flat + 1, :], 1.0)
            spectra.append(part[:, :flat].reshape(tile_rows, freq_count, half, tile_cols))
            wets.append(part[:, flat, :])
            speeds.append(physics(radian_freq, depth, dir_count)[0])
        return spectra, speeds, wets

    n_off = [-(len(below) - k) for k in range(len(below))]
    b_spec, b_speed, b_wet = unpack(below, n_off)
    north = propagate(
        jnp.concatenate(b_spec + [masked[:, :, :half]], axis=0),
        jnp.concatenate(b_speed + [group_speed], axis=0),
        jnp.concatenate(b_wet + [wet_field], axis=0),
        cosines[:half],
        sines[:half],
        True,
    )
    arrays = [(p[1], p[2]) for p in low + high]
    north, arrays = lax.optimization_barrier((north, arrays))
    tagged = [(p[0],) + tuple(a) for p, a in zip(low + high, arrays)]
    low, high = tagged[: len(low)], tagged[len(low) :]
    low_bins = [p[1] for p in reversed(low)]
    high_bins = [p[1] for p in high]
    known = {0: partial_value, far: opposite}
    for offset, _, value in low + high:
        known[offset % freq_total] = value[:, 0]
        known[(offset + far) % freq_total] = value[:, 1]
    orbital = jnp.sqrt(full_sum(known, freq_index, freq_total, partial_value))
    full_step = SUBSTEPS * sub_step
    damping = 1.0 + full_step * canopy * veg_field * orbital

    extended = jnp.concatenate(low_bins + [masked] + high_bins, axis=1)
    change = source_change(extended, quad_offsets, quad_weights, freq_count)
    increment = (masked + full_step * change) / damping[:, None, None, :] - masked

    s_off = [k + 1 for k in range(len(above))]
    a_spec, a_speed, a_wet = unpack(above, s_off)
    south = propagate(
        jnp.concatenate([masked[:, :, half:]] + a_spec, axis=0),
        jnp.concatenate([group_speed] + a_speed, axis=0),
        jnp.concatenate([wet_field] + a_wet, axis=0),
        cosines[half:],
        sines[half:],
        False,
    )
    moved = jnp.concatenate([north, south], axis=2)
    return (wet_four * (moved + increment), orbital)


def solution(mesh):
    placed = (
        P("geo", "freq", None, None),
        P("geo", None),
        P("geo", None),
        P("geo", None),
        P("geo", None),
        P(),
        P(),
    )
    return jax.shard_map(
        body,
        mesh=mesh,
        in_specs=placed,
        out_specs=(P("geo", "freq", None, None), P("geo", None)),
        check_vma=False,
    )
```

```python
import math

import jax
import jax.numpy as jnp
from jax import lax
from jax.sharding import PartitionSpec as P

FH = 4
SUBSTEPS = 8
SEND_BINS = 6


gravity = 9.81
base_freq = 0.03
freq_ratio = 1.05
cell_size = 20.0
sub_step = 2.0
coupling = 0.01
coef_plus = 0.4096
coef_minus = 3.1605
coef_both = 2.589


def from_neighbour(block, axis, distance, cyclic=False):
    count = lax.axis_size(axis)
    if cyclic:
        pairs = [(i, (i + distance) % count) for i in range(count)]
    else:
        pairs = [(i, i + distance) for i in range(count) if 0 <= i + distance < count]
    return lax.ppermute(block, axis, pairs)


def halo(block, axis, dim, width, side, cyclic=False):
    size = block.shape[dim]
    parts = []
    distance = 1
    need = width
    while need > 0:
        take = min(size, need)
        if side < 0:
            piece = lax.slice_in_dim(block, size - take, size, axis=dim)
            parts.insert(0, from_neighbour(piece, axis, distance, cyclic))
        else:
            piece = lax.slice_in_dim(block, 0, take, axis=dim)
            parts.append(from_neighbour(piece, axis, -distance, cyclic))
        need -= take
        distance += 1
    return parts


def butterfly_sum(value, axis):
    count = lax.axis_size(axis)
    assert count & (count - 1) == 0
    step = 1
    while step < count:
        value = value + lax.ppermute(value, axis, [(i, i ^ step) for i in range(count)])
        step *= 2
    return value


def gathered_sum(known, index, count, value):
    reach = max(known)
    if count > 2 * (2 * reach + 1) - 2 or count % 2:
        return butterfly_sum(value, "freq")
    far = count // 2
    ordered = jnp.stack([known[o] for o in range(-reach, reach + 1)])
    more = from_neighbour(ordered, "freq", far, True)
    table = []
    for rel in range(count):
        off = rel if rel <= reach else rel - count
        if -reach <= off <= reach:
            table.append(known[off])
        else:
            table.append(more[rel - far + reach])
    table = jnp.stack(table)
    table = jnp.concatenate([table, table], axis=0)
    start = (count - index) % count
    glob = lax.dynamic_slice_in_dim(table, start, count, axis=0)
    while glob.shape[0] > 1:
        glob = glob[0::2] + glob[1::2]
    return glob[0]


def full_sum(known, index, count, value):
    if len(known) < count or count % 2:
        return butterfly_sum(value, "freq")
    table = jnp.stack([known[rel] for rel in range(count)])
    table = jnp.concatenate([table, table], axis=0)
    glob = lax.dynamic_slice_in_dim(table, (count - index) % count, count, axis=0)
    while glob.shape[0] > 1:
        glob = glob[0::2] + glob[1::2]
    return glob[0]


def physics(radian_freq, water_depth, dir_count):
    square = (radian_freq * radian_freq)[None, :, None]
    column = water_depth[:, None, :]
    depth_ratio = square * column / gravity
    depth_wave = depth_ratio / jnp.sqrt(jnp.tanh(depth_ratio))
    group_speed = (
        radian_freq[None, :, None]
        * column
        / depth_wave
        * (0.5 + depth_wave / jnp.sinh(2.0 * depth_wave))
    )
    orbit_weight = (
        square
        / jnp.sinh(depth_wave) ** 2
        * (radian_freq * (freq_ratio - 1.0))[None, :, None]
        * (2.0 * math.pi / dir_count)
    )
    return (group_speed, orbit_weight)


def angles_of(dir_count):
    angles = (jnp.arange(dir_count, dtype=jnp.float32) + 0.5) * (2.0 * math.pi / dir_count)
    return (jnp.cos(angles), jnp.sin(angles))


def shifted(doubled, freq_start, dir_off, count):
    dir_count = doubled.shape[2] // 2
    starts = (
        jnp.zeros((), jnp.int32),
        freq_start,
        dir_off % dir_count,
        jnp.zeros((), jnp.int32),
    )
    return lax.dynamic_slice(
        doubled, starts, (doubled.shape[0], count, dir_count, doubled.shape[3])
    )


def source_change(extended, quad_offsets, quad_weights, count):
    up_bins, down_bins, up_turn, down_turn = (
        quad_offsets[0],
        quad_offsets[1],
        quad_offsets[2],
        quad_offsets[3],
    )
    weight_up, weight_down = (quad_weights[0], quad_weights[1])
    wide = count + 2 * FH
    doubled = jnp.concatenate([extended, extended], axis=2)
    centre = lax.slice_in_dim(extended, FH, FH + wide, axis=1)
    upper = weight_up * shifted(doubled, FH + up_bins, up_turn, wide) + (
        1.0 - weight_up
    ) * shifted(doubled, FH + up_bins + 1, up_turn, wide)
    lower = weight_down * shifted(doubled, FH - down_bins, -down_turn, wide) + (
        1.0 - weight_down
    ) * shifted(doubled, FH - down_bins - 1, -down_turn, wide)
    transfer = coupling * (
        centre * centre * (coef_plus * upper + coef_minus * lower)
        - coef_both * centre * upper * lower
    )
    spread = jnp.concatenate([transfer, transfer], axis=2)
    gained = weight_up * shifted(spread, FH - up_bins, -up_turn, count) + (
        1.0 - weight_up
    ) * shifted(spread, FH - up_bins - 1, -up_turn, count)
    gained = (
        gained
        + weight_down * shifted(spread, FH + down_bins, down_turn, count)
        + (1.0 - weight_down) * shifted(spread, FH + down_bins + 1, down_turn, count)
    )
    own = lax.slice_in_dim(transfer, FH, FH + count, axis=1)
    return gained - 2.0 * own


def east_west(east_flux, cosines):
    zeros = jnp.zeros_like(east_flux[..., :1])
    behind = jnp.concatenate([zeros, east_flux[..., :-1]], axis=-1)
    ahead = jnp.concatenate([east_flux[..., 1:], zeros], axis=-1)
    east_going = (cosines > 0.0)[None, None, :, None]
    return jnp.where(east_going, east_flux - behind, ahead - east_flux)


def propagate(spectrum, speed, wet, cosines, sines, northward):
    step_ratio = sub_step / cell_size
    east_speed = speed[:, :, None, :] * cosines[None, None, :, None] * step_ratio
    north_speed = speed[:, :, None, :] * sines[None, None, :, None] * step_ratio
    rows = spectrum.shape[0]
    for substep in range(SUBSTEPS):
        lo, hi = (substep, rows) if northward else (0, rows - substep)
        east_flux = east_speed[lo:hi] * spectrum
        north_flux = north_speed[lo:hi] * spectrum
        along = north_flux[1:] - north_flux[:-1]
        across = east_west(east_flux, cosines)
        if northward:
            spectrum = wet[lo + 1 : hi, None, None, :] * (
                spectrum[1:] - (across[1:] + along)
            )
        else:
            spectrum = wet[lo : hi - 1, None, None, :] * (
                spectrum[:-1] - (across[:-1] + along)
            )
    return spectrum


def body(energy, water_depth, wet_mask, vegetation, canopy, quad_offsets, quad_weights):
    tile_rows, freq_count, dir_count, tile_cols = energy.shape
    wet_field = wet_mask.astype(jnp.float32)
    veg_field = vegetation.astype(jnp.float32)
    wet_four = wet_field[:, None, None, :]
    masked = wet_four * energy
    first_bin = lax.axis_index("freq") * freq_count
    bin_index = (first_bin + jnp.arange(freq_count, dtype=jnp.int32)).astype(jnp.float32)
    radian_freq = 2.0 * math.pi * base_freq * jnp.power(freq_ratio, bin_index)
    half = dir_count // 2
    cosines, sines = angles_of(dir_count)

    fields = jnp.stack([wet_field, water_depth], axis=1)
    flat = freq_count * half
    north_msg = jnp.concatenate(
        [masked[:, :, :half].reshape(tile_rows, flat, tile_cols), fields], axis=1
    )
    south_msg = jnp.concatenate(
        [masked[:, :, half:].reshape(tile_rows, flat, tile_cols), fields], axis=1
    )
    below = halo(north_msg, "geo", 0, SUBSTEPS, -1)
    above = halo(south_msg, "geo", 0, SUBSTEPS, +1)

    group_speed, orbit_weight = physics(radian_freq, water_depth, dir_count)
    partial_value = jnp.sum(orbit_weight * jnp.sum(energy, axis=2), axis=1)

    freq_index = lax.axis_index("freq")
    freq_total = lax.axis_size("freq")
    far = freq_total // 2
    opposite = from_neighbour(partial_value, "freq", far, True)
    slot = jnp.stack([partial_value, opposite], axis=1)
    gated, slot, below, above, opposite = lax.optimization_barrier(
        (masked, slot, below, above, opposite)
    )

    def tagged_halo(side):
        pieces = []
        distance = 1
        need = 2 * FH
        while need > 0:
            take = min(freq_count, need)
            send = min(freq_count, max(take, SEND_BINS))
            lo = freq_count - send if side < 0 else 0
            cell = send * dir_count
            block = lax.slice_in_dim(gated, lo, lo + send, axis=1)
            got = from_neighbour(
                jnp.concatenate([block.reshape(tile_rows, cell, tile_cols), slot], axis=1),
                "freq",
                -side * distance,
                True,
            )
            first = send - take if side < 0 else 0
            source = freq_index + side * distance
            inside = (source >= 0) & (source < freq_total)
            bins = got[:, :cell].reshape(tile_rows, send, dir_count, tile_cols)
            pieces.append(
                (
                    distance * side,
                    jnp.where(inside, bins[:, first : first + take], 0.0),
                    got[:, cell:],
                )
            )
            need -= take
            distance += 1
        return pieces

    low = tagged_halo(-1)
    high = tagged_halo(+1)
    geo_index = lax.axis_index("geo")
    geo_count = lax.axis_size("geo")

    def unpack(parts, offsets):
        spectra, speeds, wets = [], [], []
        for part, offset in zip(parts, offsets):
            valid = (geo_index + offset >= 0) & (geo_index + offset < geo_count)
            depth = jnp.where(valid, part[:, flat + 1, :], 1.0)
            spectra.append(part[:, :flat].reshape(tile_rows, freq_count, half, tile_cols))
            wets.append(part[:, flat, :])
            speeds.append(physics(radian_freq, depth, dir_count)[0])
        return spectra, speeds, wets

    n_off = [-(len(below) - k) for k in range(len(below))]
    b_spec, b_speed, b_wet = unpack(below, n_off)
    north = propagate(
        jnp.concatenate(b_spec + [masked[:, :, :half]], axis=0),
        jnp.concatenate(b_speed + [group_speed], axis=0),
        jnp.concatenate(b_wet + [wet_field], axis=0),
        cosines[:half],
        sines[:half],
        True,
    )
    arrays = [(p[1], p[2]) for p in low + high]
    north, arrays = lax.optimization_barrier((north, arrays))
    tagged = [(p[0],) + tuple(a) for p, a in zip(low + high, arrays)]
    low, high = tagged[: len(low)], tagged[len(low) :]
    low_bins = [p[1] for p in reversed(low)]
    high_bins = [p[1] for p in high]
    known = {0: partial_value, far: opposite}
    for offset, _, value in low + high:
        known[offset % freq_total] = value[:, 0]
        known[(offset + far) % freq_total] = value[:, 1]
    orbital = jnp.sqrt(full_sum(known, freq_index, freq_total, partial_value))
    full_step = SUBSTEPS * sub_step
    damping = 1.0 + full_step * canopy * veg_field * orbital

    extended = jnp.concatenate(low_bins + [masked] + high_bins, axis=1)
    change = source_change(extended, quad_offsets, quad_weights, freq_count)
    increment = (masked + full_step * change) / damping[:, None, None, :] - masked

    s_off = [k + 1 for k in range(len(above))]
    a_spec, a_speed, a_wet = unpack(above, s_off)
    south = propagate(
        jnp.concatenate([masked[:, :, half:]] + a_spec, axis=0),
        jnp.concatenate([group_speed] + a_speed, axis=0),
        jnp.concatenate([wet_field] + a_wet, axis=0),
        cosines[half:],
        sines[half:],
        False,
    )
    moved = jnp.concatenate([north, south], axis=2)
    return (wet_four * (moved + increment), orbital)


def solution(mesh):
    placed = (
        P("geo", "freq", None, None),
        P("geo", None),
        P("geo", None),
        P("geo", None),
        P("geo", None),
        P(),
        P(),
    )
    return jax.shard_map(
        body,
        mesh=mesh,
        in_specs=placed,
        out_specs=(P("geo", "freq", None, None), P("geo", None)),
        check_vma=False,
    )
```

```python
import math

import jax
import jax.numpy as jnp
from jax import lax
from jax.sharding import PartitionSpec as P

FH = 4
SUBSTEPS = 8
SEND_BINS = 6


gravity = 9.81
base_freq = 0.03
freq_ratio = 1.05
cell_size = 20.0
sub_step = 2.0
coupling = 0.01
coef_plus = 0.4096
coef_minus = 3.1605
coef_both = 2.589


def from_neighbour(block, axis, distance, cyclic=False):
    count = lax.axis_size(axis)
    if cyclic:
        pairs = [(i, (i + distance) % count) for i in range(count)]
    else:
        pairs = [(i, i + distance) for i in range(count) if 0 <= i + distance < count]
    return lax.ppermute(block, axis, pairs)


def halo(block, axis, dim, width, side, cyclic=False):
    size = block.shape[dim]
    parts = []
    distance = 1
    need = width
    while need > 0:
        take = min(size, need)
        if side < 0:
            piece = lax.slice_in_dim(block, size - take, size, axis=dim)
            parts.insert(0, from_neighbour(piece, axis, distance, cyclic))
        else:
            piece = lax.slice_in_dim(block, 0, take, axis=dim)
            parts.append(from_neighbour(piece, axis, -distance, cyclic))
        need -= take
        distance += 1
    return parts


def butterfly_sum(value, axis):
    count = lax.axis_size(axis)
    assert count & (count - 1) == 0
    step = 1
    while step < count:
        value = value + lax.ppermute(value, axis, [(i, i ^ step) for i in range(count)])
        step *= 2
    return value


def gathered_sum(known, index, count, value):
    reach = max(known)
    if count > 2 * (2 * reach + 1) - 2 or count % 2:
        return butterfly_sum(value, "freq")
    far = count // 2
    ordered = jnp.stack([known[o] for o in range(-reach, reach + 1)])
    more = from_neighbour(ordered, "freq", far, True)
    table = []
    for rel in range(count):
        off = rel if rel <= reach else rel - count
        if -reach <= off <= reach:
            table.append(known[off])
        else:
            table.append(more[rel - far + reach])
    table = jnp.stack(table)
    table = jnp.concatenate([table, table], axis=0)
    start = (count - index) % count
    glob = lax.dynamic_slice_in_dim(table, start, count, axis=0)
    while glob.shape[0] > 1:
        glob = glob[0::2] + glob[1::2]
    return glob[0]


def full_sum(known, index, count, value):
    if len(known) < count or count % 2:
        return butterfly_sum(value, "freq")
    table = jnp.stack([known[rel] for rel in range(count)])
    table = jnp.concatenate([table, table], axis=0)
    glob = lax.dynamic_slice_in_dim(table, (count - index) % count, count, axis=0)
    while glob.shape[0] > 1:
        glob = glob[0::2] + glob[1::2]
    return glob[0]


def physics(radian_freq, water_depth, dir_count):
    square = (radian_freq * radian_freq)[None, :, None]
    column = water_depth[:, None, :]
    depth_ratio = square * column / gravity
    depth_wave = depth_ratio / jnp.sqrt(jnp.tanh(depth_ratio))
    group_speed = (
        radian_freq[None, :, None]
        * column
        / depth_wave
        * (0.5 + depth_wave / jnp.sinh(2.0 * depth_wave))
    )
    orbit_weight = (
        square
        / jnp.sinh(depth_wave) ** 2
        * (radian_freq * (freq_ratio - 1.0))[None, :, None]
        * (2.0 * math.pi / dir_count)
    )
    return (group_speed, orbit_weight)


def angles_of(dir_count):
    angles = (jnp.arange(dir_count, dtype=jnp.float32) + 0.5) * (2.0 * math.pi / dir_count)
    return (jnp.cos(angles), jnp.sin(angles))


def shifted(doubled, freq_start, dir_off, count):
    dir_count = doubled.shape[2] // 2
    starts = (
        jnp.zeros((), jnp.int32),
        freq_start,
        dir_off % dir_count,
        jnp.zeros((), jnp.int32),
    )
    return lax.dynamic_slice(
        doubled, starts, (doubled.shape[0], count, dir_count, doubled.shape[3])
    )


def source_change(extended, quad_offsets, quad_weights, count):
    up_bins, down_bins, up_turn, down_turn = (
        quad_offsets[0],
        quad_offsets[1],
        quad_offsets[2],
        quad_offsets[3],
    )
    weight_up, weight_down = (quad_weights[0], quad_weights[1])
    wide = count + 2 * FH
    doubled = jnp.concatenate([extended, extended], axis=2)
    centre = lax.slice_in_dim(extended, FH, FH + wide, axis=1)
    upper = weight_up * shifted(doubled, FH + up_bins, up_turn, wide) + (
        1.0 - weight_up
    ) * shifted(doubled, FH + up_bins + 1, up_turn, wide)
    lower = weight_down * shifted(doubled, FH - down_bins, -down_turn, wide) + (
        1.0 - weight_down
    ) * shifted(doubled, FH - down_bins - 1, -down_turn, wide)
    transfer = coupling * (
        centre * centre * (coef_plus * upper + coef_minus * lower)
        - coef_both * centre * upper * lower
    )
    spread = jnp.concatenate([transfer, transfer], axis=2)
    gained = weight_up * shifted(spread, FH - up_bins, -up_turn, count) + (
        1.0 - weight_up
    ) * shifted(spread, FH - up_bins - 1, -up_turn, count)
    gained = (
        gained
        + weight_down * shifted(spread, FH + down_bins, down_turn, count)
        + (1.0 - weight_down) * shifted(spread, FH + down_bins + 1, down_turn, count)
    )
    own = lax.slice_in_dim(transfer, FH, FH + count, axis=1)
    return gained - 2.0 * own


def east_west(east_flux, cosines):
    zeros = jnp.zeros_like(east_flux[..., :1])
    behind = jnp.concatenate([zeros, east_flux[..., :-1]], axis=-1)
    ahead = jnp.concatenate([east_flux[..., 1:], zeros], axis=-1)
    east_going = (cosines > 0.0)[None, None, :, None]
    return jnp.where(east_going, east_flux - behind, ahead - east_flux)


def propagate(spectrum, speed, wet, cosines, sines, northward):
    step_ratio = sub_step / cell_size
    east_speed = speed[:, :, None, :] * cosines[None, None, :, None] * step_ratio
    north_speed = speed[:, :, None, :] * sines[None, None, :, None] * step_ratio
    rows = spectrum.shape[0]
    for substep in range(SUBSTEPS):
        lo, hi = (substep, rows) if northward else (0, rows - substep)
        east_flux = east_speed[lo:hi] * spectrum
        north_flux = north_speed[lo:hi] * spectrum
        along = north_flux[1:] - north_flux[:-1]
        across = east_west(east_flux, cosines)
        if northward:
            spectrum = wet[lo + 1 : hi, None, None, :] * (
                spectrum[1:] - (across[1:] + along)
            )
        else:
            spectrum = wet[lo : hi - 1, None, None, :] * (
                spectrum[:-1] - (across[:-1] + along)
            )
    return spectrum


def body(energy, water_depth, wet_mask, vegetation, canopy, quad_offsets, quad_weights):
    tile_rows, freq_count, dir_count, tile_cols = energy.shape
    wet_field = wet_mask.astype(jnp.float32)
    veg_field = vegetation.astype(jnp.float32)
    wet_four = wet_field[:, None, None, :]
    masked = wet_four * energy
    first_bin = lax.axis_index("freq") * freq_count
    bin_index = (first_bin + jnp.arange(freq_count, dtype=jnp.int32)).astype(jnp.float32)
    radian_freq = 2.0 * math.pi * base_freq * jnp.power(freq_ratio, bin_index)
    half = dir_count // 2
    cosines, sines = angles_of(dir_count)

    fields = jnp.stack([wet_field, water_depth], axis=1)
    flat = freq_count * half
    north_msg = jnp.concatenate(
        [masked[:, :, :half].reshape(tile_rows, flat, tile_cols), fields], axis=1
    )
    south_msg = jnp.concatenate(
        [masked[:, :, half:].reshape(tile_rows, flat, tile_cols), fields], axis=1
    )
    below = halo(north_msg, "geo", 0, SUBSTEPS, -1)
    above = halo(south_msg, "geo", 0, SUBSTEPS, +1)

    group_speed, orbit_weight = physics(radian_freq, water_depth, dir_count)
    partial_value = jnp.sum(orbit_weight * jnp.sum(energy, axis=2), axis=1)

    freq_index = lax.axis_index("freq")
    freq_total = lax.axis_size("freq")
    far = freq_total // 2
    opposite = from_neighbour(partial_value, "freq", far, True)
    slot = jnp.stack([partial_value, opposite], axis=1)
    gated, slot, below, above, opposite = lax.optimization_barrier(
        (masked, slot, below, above, opposite)
    )

    def tagged_halo(side):
        pieces = []
        distance = 1
        need = 2 * FH
        while need > 0:
            take = min(freq_count, need)
            send = min(freq_count, max(take, SEND_BINS))
            lo = freq_count - send if side < 0 else 0
            cell = send * dir_count
            block = lax.slice_in_dim(gated, lo, lo + send, axis=1)
            got = from_neighbour(
                jnp.concatenate([block.reshape(tile_rows, cell, tile_cols), slot], axis=1),
                "freq",
                -side * distance,
                True,
            )
            first = send - take if side < 0 else 0
            source = freq_index + side * distance
            inside = (source >= 0) & (source < freq_total)
            bins = got[:, :cell].reshape(tile_rows, send, dir_count, tile_cols)
            pieces.append(
                (
                    distance * side,
                    jnp.where(inside, bins[:, first : first + take], 0.0),
                    got[:, cell:],
                )
            )
            need -= take
            distance += 1
        return pieces

    low = tagged_halo(-1)
    high = tagged_halo(+1)
    geo_index = lax.axis_index("geo")
    geo_count = lax.axis_size("geo")

    def unpack(parts, offsets):
        spectra, speeds, wets = [], [], []
        for part, offset in zip(parts, offsets):
            valid = (geo_index + offset >= 0) & (geo_index + offset < geo_count)
            depth = jnp.where(valid, part[:, flat + 1, :], 1.0)
            spectra.append(part[:, :flat].reshape(tile_rows, freq_count, half, tile_cols))
            wets.append(part[:, flat, :])
            speeds.append(physics(radian_freq, depth, dir_count)[0])
        return spectra, speeds, wets

    n_off = [-(len(below) - k) for k in range(len(below))]
    b_spec, b_speed, b_wet = unpack(below, n_off)
    north = propagate(
        jnp.concatenate(b_spec + [masked[:, :, :half]], axis=0),
        jnp.concatenate(b_speed + [group_speed], axis=0),
        jnp.concatenate(b_wet + [wet_field], axis=0),
        cosines[:half],
        sines[:half],
        True,
    )
    arrays = [(p[1], p[2]) for p in low + high]
    north, arrays = lax.optimization_barrier((north, arrays))
    tagged = [(p[0],) + tuple(a) for p, a in zip(low + high, arrays)]
    low, high = tagged[: len(low)], tagged[len(low) :]
    low_bins = [p[1] for p in reversed(low)]
    high_bins = [p[1] for p in high]
    known = {0: partial_value, far: opposite}
    for offset, _, value in low + high:
        known[offset % freq_total] = value[:, 0]
        known[(offset + far) % freq_total] = value[:, 1]
    orbital = jnp.sqrt(full_sum(known, freq_index, freq_total, partial_value))
    full_step = SUBSTEPS * sub_step
    damping = 1.0 + full_step * canopy * veg_field * orbital

    extended = jnp.concatenate(low_bins + [masked] + high_bins, axis=1)
    change = source_change(extended, quad_offsets, quad_weights, freq_count)
    relief = 1.0 / damping
    increment = (masked + full_step * change) * relief[:, None, None, :] - masked

    s_off = [k + 1 for k in range(len(above))]
    a_spec, a_speed, a_wet = unpack(above, s_off)
    south = propagate(
        jnp.concatenate([masked[:, :, half:]] + a_spec, axis=0),
        jnp.concatenate([group_speed] + a_speed, axis=0),
        jnp.concatenate([wet_field] + a_wet, axis=0),
        cosines[half:],
        sines[half:],
        False,
    )
    moved = jnp.concatenate([north, south], axis=2)
    return (wet_four * (moved + increment), orbital)


def solution(mesh):
    placed = (
        P("geo", "freq", None, None),
        P("geo", None),
        P("geo", None),
        P("geo", None),
        P("geo", None),
        P(),
        P(),
    )
    return jax.shard_map(
        body,
        mesh=mesh,
        in_specs=placed,
        out_specs=(P("geo", "freq", None, None), P("geo", None)),
        check_vma=False,
    )
```

```python
import math

import jax
import jax.numpy as jnp
import numpy as np
from jax import lax
from jax.sharding import PartitionSpec as P

FH = 4
SUBSTEPS = 8
SEND_BINS = 6


gravity = 9.81
base_freq = 0.03
freq_ratio = 1.05
cell_size = 20.0
sub_step = 2.0
coupling = 0.01
coef_plus = 0.4096
coef_minus = 3.1605
coef_both = 2.589


def from_neighbour(block, axis, distance, cyclic=False):
    count = lax.axis_size(axis)
    if cyclic:
        pairs = [(i, (i + distance) % count) for i in range(count)]
    else:
        pairs = [(i, i + distance) for i in range(count) if 0 <= i + distance < count]
    return lax.ppermute(block, axis, pairs)


def halo(block, axis, dim, width, side, cyclic=False):
    size = block.shape[dim]
    parts = []
    distance = 1
    need = width
    while need > 0:
        take = min(size, need)
        if side < 0:
            piece = lax.slice_in_dim(block, size - take, size, axis=dim)
            parts.insert(0, from_neighbour(piece, axis, distance, cyclic))
        else:
            piece = lax.slice_in_dim(block, 0, take, axis=dim)
            parts.append(from_neighbour(piece, axis, -distance, cyclic))
        need -= take
        distance += 1
    return parts


def butterfly_sum(value, axis):
    count = lax.axis_size(axis)
    assert count & (count - 1) == 0
    step = 1
    while step < count:
        value = value + lax.ppermute(value, axis, [(i, i ^ step) for i in range(count)])
        step *= 2
    return value


def gathered_sum(known, index, count, value):
    reach = max(known)
    if count > 2 * (2 * reach + 1) - 2 or count % 2:
        return butterfly_sum(value, "freq")
    far = count // 2
    ordered = jnp.stack([known[o] for o in range(-reach, reach + 1)])
    more = from_neighbour(ordered, "freq", far, True)
    table = []
    for rel in range(count):
        off = rel if rel <= reach else rel - count
        if -reach <= off <= reach:
            table.append(known[off])
        else:
            table.append(more[rel - far + reach])
    table = jnp.stack(table)
    table = jnp.concatenate([table, table], axis=0)
    start = (count - index) % count
    glob = lax.dynamic_slice_in_dim(table, start, count, axis=0)
    while glob.shape[0] > 1:
        glob = glob[0::2] + glob[1::2]
    return glob[0]


def full_sum(known, index, count, value):
    if len(known) < count or count % 2:
        return butterfly_sum(value, "freq")
    table = jnp.stack([known[rel] for rel in range(count)])
    table = jnp.concatenate([table, table], axis=0)
    glob = lax.dynamic_slice_in_dim(table, (count - index) % count, count, axis=0)
    while glob.shape[0] > 1:
        glob = glob[0::2] + glob[1::2]
    return glob[0]


def physics(radian_freq, water_depth, dir_count):
    square = (radian_freq * radian_freq)[None, :, None]
    column = water_depth[:, None, :]
    depth_ratio = square * column / gravity
    depth_wave = depth_ratio / jnp.sqrt(jnp.tanh(depth_ratio))
    group_speed = (
        radian_freq[None, :, None]
        * column
        / depth_wave
        * (0.5 + depth_wave / jnp.sinh(2.0 * depth_wave))
    )
    orbit_weight = (
        square
        / jnp.sinh(depth_wave) ** 2
        * (radian_freq * (freq_ratio - 1.0))[None, :, None]
        * (2.0 * math.pi / dir_count)
    )
    return (group_speed, orbit_weight)


def angles_of(dir_count):
    angles = (jnp.arange(dir_count, dtype=jnp.float32) + 0.5) * (2.0 * math.pi / dir_count)
    return (jnp.cos(angles), jnp.sin(angles))


def shifted(doubled, freq_start, dir_off, count):
    dir_count = doubled.shape[2] // 2
    starts = (
        jnp.zeros((), jnp.int32),
        freq_start,
        dir_off % dir_count,
        jnp.zeros((), jnp.int32),
    )
    return lax.dynamic_slice(
        doubled, starts, (doubled.shape[0], count, dir_count, doubled.shape[3])
    )


def source_change(extended, quad_offsets, quad_weights, count):
    up_bins, down_bins, up_turn, down_turn = (
        quad_offsets[0],
        quad_offsets[1],
        quad_offsets[2],
        quad_offsets[3],
    )
    weight_up, weight_down = (quad_weights[0], quad_weights[1])
    wide = count + 2 * FH
    doubled = jnp.concatenate([extended, extended], axis=2)
    centre = lax.slice_in_dim(extended, FH, FH + wide, axis=1)
    upper = weight_up * shifted(doubled, FH + up_bins, up_turn, wide) + (
        1.0 - weight_up
    ) * shifted(doubled, FH + up_bins + 1, up_turn, wide)
    lower = weight_down * shifted(doubled, FH - down_bins, -down_turn, wide) + (
        1.0 - weight_down
    ) * shifted(doubled, FH - down_bins - 1, -down_turn, wide)
    transfer = coupling * (
        centre * centre * (coef_plus * upper + coef_minus * lower)
        - coef_both * centre * upper * lower
    )
    spread = jnp.concatenate([transfer, transfer], axis=2)
    gained = weight_up * shifted(spread, FH - up_bins, -up_turn, count) + (
        1.0 - weight_up
    ) * shifted(spread, FH - up_bins - 1, -up_turn, count)
    gained = (
        gained
        + weight_down * shifted(spread, FH + down_bins, down_turn, count)
        + (1.0 - weight_down) * shifted(spread, FH + down_bins + 1, down_turn, count)
    )
    own = lax.slice_in_dim(transfer, FH, FH + count, axis=1)
    return gained - 2.0 * own


def east_west(east_flux, cosines):
    zeros = jnp.zeros_like(east_flux[..., :1])
    behind = jnp.concatenate([zeros, east_flux[..., :-1]], axis=-1)
    ahead = jnp.concatenate([east_flux[..., 1:], zeros], axis=-1)
    east_going = (cosines > 0.0)[None, None, :, None]
    return jnp.where(east_going, east_flux - behind, ahead - east_flux)


def upwind_across(east_flux, east_static):
    parts = []
    start = 0
    for stop in range(1, len(east_static) + 1):
        if stop < len(east_static) and east_static[stop] == east_static[start]:
            continue
        flux = east_flux[:, :, start:stop]
        zeros = jnp.zeros_like(flux[..., :1])
        if east_static[start]:
            parts.append(flux - jnp.concatenate([zeros, flux[..., :-1]], axis=-1))
        else:
            parts.append(jnp.concatenate([flux[..., 1:], zeros], axis=-1) - flux)
        start = stop
    return jnp.concatenate(parts, axis=2) if len(parts) > 1 else parts[0]


def propagate(spectrum, speed, wet, cosines, sines, northward, east_static):
    step_ratio = sub_step / cell_size
    east_speed = speed[:, :, None, :] * cosines[None, None, :, None] * step_ratio
    north_speed = speed[:, :, None, :] * sines[None, None, :, None] * step_ratio
    rows = spectrum.shape[0]
    for substep in range(SUBSTEPS):
        lo, hi = (substep, rows) if northward else (0, rows - substep)
        east_flux = east_speed[lo:hi] * spectrum
        north_flux = north_speed[lo:hi] * spectrum
        along = north_flux[1:] - north_flux[:-1]
        across = upwind_across(east_flux, east_static)
        if northward:
            spectrum = wet[lo + 1 : hi, None, None, :] * (
                spectrum[1:] - (across[1:] + along)
            )
        else:
            spectrum = wet[lo : hi - 1, None, None, :] * (
                spectrum[:-1] - (across[:-1] + along)
            )
    return spectrum


def body(energy, water_depth, wet_mask, vegetation, canopy, quad_offsets, quad_weights):
    tile_rows, freq_count, dir_count, tile_cols = energy.shape
    wet_field = wet_mask.astype(jnp.float32)
    veg_field = vegetation.astype(jnp.float32)
    wet_four = wet_field[:, None, None, :]
    masked = wet_four * energy
    first_bin = lax.axis_index("freq") * freq_count
    bin_index = (first_bin + jnp.arange(freq_count, dtype=jnp.int32)).astype(jnp.float32)
    radian_freq = 2.0 * math.pi * base_freq * jnp.power(freq_ratio, bin_index)
    half = dir_count // 2
    cosines, sines = angles_of(dir_count)
    east_static = np.cos((np.arange(dir_count) + 0.5) * (2.0 * math.pi / dir_count)) > 0.0

    fields = jnp.stack([wet_field, water_depth], axis=1)
    flat = freq_count * half
    north_msg = jnp.concatenate(
        [masked[:, :, :half].reshape(tile_rows, flat, tile_cols), fields], axis=1
    )
    south_msg = jnp.concatenate(
        [masked[:, :, half:].reshape(tile_rows, flat, tile_cols), fields], axis=1
    )
    below = halo(north_msg, "geo", 0, SUBSTEPS, -1)
    above = halo(south_msg, "geo", 0, SUBSTEPS, +1)

    group_speed, orbit_weight = physics(radian_freq, water_depth, dir_count)
    partial_value = jnp.sum(orbit_weight * jnp.sum(energy, axis=2), axis=1)

    freq_index = lax.axis_index("freq")
    freq_total = lax.axis_size("freq")
    far = freq_total // 2
    opposite = from_neighbour(partial_value, "freq", far, True)
    slot = jnp.stack([partial_value, opposite], axis=1)
    gated, slot, below, above, opposite = lax.optimization_barrier(
        (masked, slot, below, above, opposite)
    )

    def tagged_halo(side):
        pieces = []
        distance = 1
        need = 2 * FH
        while need > 0:
            take = min(freq_count, need)
            send = min(freq_count, max(take, SEND_BINS))
            lo = freq_count - send if side < 0 else 0
            cell = send * dir_count
            block = lax.slice_in_dim(gated, lo, lo + send, axis=1)
            got = from_neighbour(
                jnp.concatenate([block.reshape(tile_rows, cell, tile_cols), slot], axis=1),
                "freq",
                -side * distance,
                True,
            )
            first = send - take if side < 0 else 0
            source = freq_index + side * distance
            inside = (source >= 0) & (source < freq_total)
            bins = got[:, :cell].reshape(tile_rows, send, dir_count, tile_cols)
            pieces.append(
                (
                    distance * side,
                    jnp.where(inside, bins[:, first : first + take], 0.0),
                    got[:, cell:],
                )
            )
            need -= take
            distance += 1
        return pieces

    low = tagged_halo(-1)
    high = tagged_halo(+1)
    geo_index = lax.axis_index("geo")
    geo_count = lax.axis_size("geo")

    def unpack(parts, offsets):
        spectra, speeds, wets = [], [], []
        for part, offset in zip(parts, offsets):
            valid = (geo_index + offset >= 0) & (geo_index + offset < geo_count)
            depth = jnp.where(valid, part[:, flat + 1, :], 1.0)
            spectra.append(part[:, :flat].reshape(tile_rows, freq_count, half, tile_cols))
            wets.append(part[:, flat, :])
            speeds.append(physics(radian_freq, depth, dir_count)[0])
        return spectra, speeds, wets

    n_off = [-(len(below) - k) for k in range(len(below))]
    b_spec, b_speed, b_wet = unpack(below, n_off)
    north = propagate(
        jnp.concatenate(b_spec + [masked[:, :, :half]], axis=0),
        jnp.concatenate(b_speed + [group_speed], axis=0),
        jnp.concatenate(b_wet + [wet_field], axis=0),
        cosines[:half],
        sines[:half],
        True,
        east_static[:half],
    )
    arrays = [(p[1], p[2]) for p in low + high]
    north, arrays = lax.optimization_barrier((north, arrays))
    tagged = [(p[0],) + tuple(a) for p, a in zip(low + high, arrays)]
    low, high = tagged[: len(low)], tagged[len(low) :]
    low_bins = [p[1] for p in reversed(low)]
    high_bins = [p[1] for p in high]
    known = {0: partial_value, far: opposite}
    for offset, _, value in low + high:
        known[offset % freq_total] = value[:, 0]
        known[(offset + far) % freq_total] = value[:, 1]
    orbital = jnp.sqrt(full_sum(known, freq_index, freq_total, partial_value))
    full_step = SUBSTEPS * sub_step
    damping = 1.0 + full_step * canopy * veg_field * orbital

    extended = jnp.concatenate(low_bins + [masked] + high_bins, axis=1)
    change = source_change(extended, quad_offsets, quad_weights, freq_count)
    increment = (masked + full_step * change) / damping[:, None, None, :] - masked

    s_off = [k + 1 for k in range(len(above))]
    a_spec, a_speed, a_wet = unpack(above, s_off)
    south = propagate(
        jnp.concatenate([masked[:, :, half:]] + a_spec, axis=0),
        jnp.concatenate([group_speed] + a_speed, axis=0),
        jnp.concatenate([wet_field] + a_wet, axis=0),
        cosines[half:],
        sines[half:],
        False,
        east_static[half:],
    )
    moved = jnp.concatenate([north, south], axis=2)
    return (wet_four * (moved + increment), orbital)


def solution(mesh):
    placed = (
        P("geo", "freq", None, None),
        P("geo", None),
        P("geo", None),
        P("geo", None),
        P("geo", None),
        P(),
        P(),
    )
    return jax.shard_map(
        body,
        mesh=mesh,
        in_specs=placed,
        out_specs=(P("geo", "freq", None, None), P("geo", None)),
        check_vma=False,
    )
```
